128 devices in a mesh: tm: 16 (over x, y), od: 8 (over z, core).
Axes of the slice: x: 4, y: 4, z: 4, core: 2. Of those that a mesh axis runs over, the one named last changes fastest.
Arguments:
- tiles: bfloat16 [256, 360, 128, 128], P('tm', 'od'), may hold values from -6 to 6
- coords: int32 [2, 256, 360], P(None, 'tm', 'od'), may hold values from 0 to 31
- counts: int32 [256, 8], P('tm', 'od'), may hold values from 1 to 45, as said below
- anchor_factor: bfloat16 [4096, 256], P(('tm', 'od')), may hold values from -0.375 to 0.375
- dest_factor: bfloat16 [4096, 256], P(('tm', 'od')), may hold values from -0.375 to 0.375
- filter_trans: float32 [256, 256], replicated, may hold values from -1 to 1
- filter_gain: float32 [256, 256], replicated, may hold values from -1 to 1
- transition: float32 [256, 256], replicated, may hold values from -1 to 1
- smooth_gain: float32 [256, 256], replicated, may hold values from -1 to 1
Outputs:
- filtered: float32 [256, 256], P('tm')
- smoothed: float32 [256, 256], P('tm')
The draws below stay inside these ranges and needn't reach their ends.
Inputs may be any that keep to these rules, and one draw needn't show every extreme that they name: `counts`: in every draw some step on some index of od has all 45 slots live.
All inputs are finite; a program needn't handle non-finite values.
Results may differ from the reference program's by a relative error of at most 0.0003.
Values may be sent and summed in bfloat16 or wider, within the bound.
No kernel may reach another device: no remote copies, remote signals or barrier semaphores. Data moves between devices by JAX's collectives and lax.ppermute only.
A program may use at most 192 MiB of HBM per device.

```python
import jax
import jax.numpy as jnp
from jax import lax

R = 256
TILE = 128
SLOT_DEV = 45
WINDOW = 256
SLOTS = 360
ZONES = 4096
ZTILES = 32
N_OD = 8


def rate_draw(key, slow_share):
    pick_key, slow_key, fast_key = jax.random.split(key, 3)
    slow_mask = jax.random.uniform(pick_key, (R,)) < slow_share
    slow_rate = jnp.exp(-1.0 / (WINDOW * jax.random.uniform(slow_key, (R,), minval=0.45, maxval=2.0)))
    fast_rate = jnp.exp(-1.0 / jax.random.uniform(fast_key, (R,), minval=20.0, maxval=40.0))
    return jnp.where(slow_mask, slow_rate, fast_rate)


def slow_share_value():
    share = 0.5
    return share


def mixing(key, rates):
    spread = jax.random.uniform(key, (R, R), minval=-1.0, maxval=1.0)
    eye_mask = jnp.eye(R, dtype=jnp.float32)
    return (1.0 - eye_mask) * spread * ((1.0 - rates) / R)[:, None] + eye_mask * rates[:, None]


def draw_filter_trans(key, part):
    rates = rate_draw(jax.random.fold_in(key, 11), slow_share_value())
    return mixing(jax.random.fold_in(key, 12), rates)


def draw_filter_gain(key, part):
    rates = rate_draw(jax.random.fold_in(key, 11), slow_share_value())
    noise_key = jax.random.fold_in(key, 13)
    noise = jax.random.truncated_normal(noise_key, -4.0, 4.0, (R, R))
    scaled = noise * jnp.sqrt(1.0 - rates * rates)[:, None] / jnp.sqrt(R * 1.0)
    return jnp.clip(scaled, -1.0, 1.0)


def draw_smooth_gain(key, part):
    rates = rate_draw(jax.random.fold_in(key, 21), slow_share_value())
    return mixing(jax.random.fold_in(key, 22), rates)


def draw_transition(key, part):
    rates = 1.0 - jax.random.uniform(jax.random.fold_in(key, 31), (R,), minval=0.0005, maxval=0.004)
    return mixing(jax.random.fold_in(key, 32), rates)


def draw_counts(key, part):
    high_key, pick_key, value_key, spot_key = jax.random.split(key, 4)
    least_top = min(max(SLOT_DEV // 4, 2), SLOT_DEV)
    tops = jax.random.randint(high_key, (N_OD,), least_top, SLOT_DEV + 1)
    busy = jax.random.randint(pick_key, (), 0, N_OD)
    tops = jnp.where(jnp.arange(N_OD) == busy, SLOT_DEV, tops)
    lower = tops // 3
    raw_bits = jax.random.randint(value_key, (WINDOW, N_OD), 0, 1 << 20)
    counts = lower[None, :] + 1 + raw_bits % jnp.maximum(tops - lower, 1)[None, :]
    spot = jax.random.randint(spot_key, (), 0, WINDOW)
    return counts.at[spot, busy].set(SLOT_DEV).astype(jnp.int32)


def touch_ends(drawn, own_key, smallest, top_value):
    longest = drawn.shape.index(max(drawn.shape))
    spots = []
    for shift in (0, 1):
        where = [jax.random.randint(jax.random.fold_in(own_key, axis), (), 0, length) for axis, length in enumerate(drawn.shape)]
        where[longest] = (where[longest] + shift) % drawn.shape[longest]
        spots.append(tuple(where))
    return drawn.at[spots[0]].set(smallest).at[spots[1]].set(top_value)


def level_of(rng, dims, pieces, low, high):
    level = 1.0
    for position, shards_of in pieces:
        steps = jax.random.uniform(jax.random.fold_in(jax.random.fold_in(rng, 6), position), (shards_of,), jnp.float32, low / len(pieces), high / len(pieces))
        level = level * jnp.repeat(jnp.exp(steps), dims[position] // shards_of).reshape((-1,) + (1,) * (len(dims) - 1 - position))
    return level


def bell_draw(own_key, extent, scale, most, cuts=(), kind=jnp.bfloat16):
    result = jax.random.normal(own_key, extent, jnp.float32) * scale
    if len(cuts) > 0:
        result = level_of(own_key, extent, cuts, -0.22, 0.18) * result
    return jnp.clip(result, min=-most, max=most).astype(kind)


def setup_inputs(seed: int = 0) -> dict:
    seeds = jax.random.split(jax.random.key(seed), 10)
    tiles = bell_draw(seeds[0], (WINDOW, SLOTS, TILE, TILE), 1.0, 6.0, ((0, 16), (1, 8)))
    coords = touch_ends(jax.random.randint(seeds[1], (2, WINDOW, SLOTS), 0, ZTILES), jax.random.fold_in(seeds[1], 1), 0, ZTILES - 1).astype(jnp.int32)
    counts = draw_counts(jax.random.fold_in(seeds[9], 71), 0)
    anchor_factor = bell_draw(seeds[3], (ZONES, R), (1.0 / (SLOTS * TILE * TILE / 2) ** 0.25), 0.375, ((0, 128),))
    dest_factor = bell_draw(seeds[4], (ZONES, R), (1.0 / (SLOTS * TILE * TILE / 2) ** 0.25), 0.375, ((0, 128),))
    filter_trans = draw_filter_trans(jax.random.fold_in(seeds[9], 71), 0)
    filter_gain = draw_filter_gain(jax.random.fold_in(seeds[9], 71), 0)
    transition = draw_transition(jax.random.fold_in(seeds[9], 71), 0)
    smooth_gain = draw_smooth_gain(jax.random.fold_in(seeds[9], 71), 0)
    return dict(tiles=tiles, coords=coords, counts=counts, anchor_factor=anchor_factor, dest_factor=dest_factor, filter_trans=filter_trans, filter_gain=filter_gain, transition=transition, smooth_gain=smooth_gain)


HIGHEST = lax.Precision.HIGHEST


def reference(tiles, coords, counts, anchor_factor, dest_factor, filter_trans, filter_gain, transition, smooth_gain):
    orig_tiles = anchor_factor.astype(jnp.float32).reshape(-1, TILE, R)
    dest_tiles = dest_factor.astype(jnp.float32).reshape(-1, TILE, R)
    slot_ids = jnp.arange(SLOTS, dtype=jnp.int32)

    def one_step(inputs):
        tile_block, orig_ids, dest_ids, step_counts = inputs
        live_mask = (slot_ids % SLOT_DEV < step_counts[slot_ids // SLOT_DEV]).astype(jnp.float32)
        tile_dest = jnp.einsum("sij,sjr->sir", tile_block.astype(jnp.float32), dest_tiles[dest_ids])
        return jnp.sum(tile_dest * orig_tiles[orig_ids] * live_mask[:, None, None], axis=(0, 1))

    observed = lax.map(one_step, (tiles, coords[0], coords[1], counts))
    drive = jnp.dot(observed, filter_gain.T, precision=HIGHEST)

    def forward_step(carried, drive_row):
        updated = jnp.dot(filter_trans, carried, precision=HIGHEST) + drive_row
        return updated, updated

    final_state, filtered = lax.scan(forward_step, jnp.zeros((R,), jnp.float32), drive)
    predicted = jnp.dot(filtered, transition.T, precision=HIGHEST)
    back_terms = filtered - jnp.dot(predicted, smooth_gain.T, precision=HIGHEST)
    back_terms = back_terms.at[WINDOW - 1].set(filtered[WINDOW - 1])

    def backward_step(carried, back_row):
        updated = jnp.dot(smooth_gain, carried, precision=HIGHEST) + back_row
        return updated, updated

    first_state, smoothed = lax.scan(backward_step, jnp.zeros((R,), jnp.float32), back_terms, reverse=True)
    return filtered, smoothed
```

```python
import jax
import jax.numpy as jnp
from jax import lax
from jax.sharding import PartitionSpec as P
from jax.experimental import pallas as pl
from jax.experimental.pallas import tpu as pltpu

HIGHEST = lax.Precision.HIGHEST


def joined_along(pieces, dim):
    shape = list(pieces.shape[1:])
    shape[dim] *= pieces.shape[0]
    return jnp.moveaxis(pieces, 0, dim).reshape(shape)


def from_everyone(array, axis):
    size = lax.axis_size(axis)
    return lax.all_to_all(
        jnp.broadcast_to(array[None], (size, *array.shape)), axis, 0, 0, tiled=True
    )


def collect(array, axis, dim):
    return joined_along(from_everyone(array, axis), dim)


def in_one_piece(arrays, axis, dim, along):
    widths = [a.shape[along] for a in arrays]
    both = jnp.concatenate(arrays, axis=along)
    filled = lax.all_gather(both, axis, axis=dim, tiled=True)
    return tuple(jnp.split(filled, [sum(widths[:k]) for k in range(1, len(widths))], axis=along))


def over_copies(array, axis):
    everything = from_everyone(array, axis)
    return jnp.sum(everything, axis=0)


def product(left_mat, right_mat):
    return jnp.dot(left_mat, right_mat, precision=HIGHEST)


def matrix_power(matrix, exponent):
    result = None
    squared = matrix
    while exponent > 0:
        if exponent % 2 == 1:
            result = squared
        exponent = exponent // 2
        if exponent > 0:
            squared = product(squared, squared)
    return result


def run_rows(start_state, drive, matrix, reverse):

    def advance(carried, drive_row):
        updated = jnp.dot(matrix, carried, precision=HIGHEST) + drive_row
        return (updated, updated)

    return lax.scan(advance, start_state, drive, reverse=reverse)[1]


def backward_terms(filtered, transition, smooth_gain, last_device):
    predicted = product(filtered, transition.T)
    back_terms = filtered - product(predicted, smooth_gain.T)
    row_ids = lax.broadcasted_iota(jnp.int32, back_terms.shape, 0)
    final_row = jnp.logical_and(last_device, row_ids == back_terms.shape[0] - 1)
    return jnp.where(final_row, filtered, back_terms)


def forward_start(stride, last_state):
    states = collect(last_state[None], "tm", 0)
    own_index = lax.axis_index("tm")

    def forward_horner_step(position, running):
        stepped = jnp.dot(stride, running, precision=HIGHEST) + states[position]
        return jnp.where(position < own_index, stepped, running)

    return lax.fori_loop(0, lax.axis_size("tm"), forward_horner_step, jnp.zeros_like(last_state))


def backward_start(stride, first_state):
    states = collect(first_state[None], "tm", 0)
    own_index = lax.axis_index("tm")
    group_size = lax.axis_size("tm")

    def backward_horner_step(turn, running):
        position = group_size - 1 - turn
        stepped = jnp.dot(stride, running, precision=HIGHEST) + states[position]
        return jnp.where(position > own_index, stepped, running)

    return lax.fori_loop(0, group_size, backward_horner_step, jnp.zeros_like(first_state))


def mttkrp_kernel(coords_ref, counts_ref, tiles_ref, anchor_ref, dest_ref, out_ref):
    step = pl.program_id(0)
    slot_total = tiles_ref.shape[1]
    tile_side = tiles_ref.shape[2]
    tile_top = anchor_ref.shape[0] // tile_side - 1
    live = jnp.clip(counts_ref[step], 0, slot_total)

    def one_slot(slot, acc):
        orig_id = jnp.clip(coords_ref[0, step, slot], 0, tile_top)
        dest_id = jnp.clip(coords_ref[1, step, slot], 0, tile_top)
        dest_rows = dest_ref[pl.ds(pl.multiple_of(dest_id * tile_side, tile_side), tile_side), :]
        orig_rows = anchor_ref[pl.ds(pl.multiple_of(orig_id * tile_side, tile_side), tile_side), :]
        tile_dest = jnp.dot(tiles_ref[0, slot], dest_rows, preferred_element_type=jnp.float32)
        return acc + tile_dest * orig_rows.astype(jnp.float32)

    acc = lax.fori_loop(
        0, live, one_slot, jnp.zeros((tile_side, anchor_ref.shape[1]), jnp.float32)
    )
    out_ref[0] = jnp.sum(acc, axis=0, keepdims=True)


def mttkrp(tiles, coords, live_counts, orig_all, dest_all):
    step_count, slot_count, tile_side, _ = tiles.shape
    state_width = orig_all.shape[1]
    grid_spec = pltpu.PrefetchScalarGridSpec(
        num_scalar_prefetch=2,
        grid=(step_count,),
        in_specs=[
            pl.BlockSpec((1, slot_count, tile_side, tile_side), lambda t, c, n: (t, 0, 0, 0)),
            pl.BlockSpec(orig_all.shape, lambda t, c, n: (0, 0)),
            pl.BlockSpec(dest_all.shape, lambda t, c, n: (0, 0)),
        ],
        out_specs=pl.BlockSpec((1, 1, state_width), lambda t, c, n: (t, 0, 0)),
    )
    out = pl.pallas_call(
        mttkrp_kernel,
        grid_spec=grid_spec,
        out_shape=jax.ShapeDtypeStruct((step_count, 1, state_width), jnp.float32),
        compiler_params=pltpu.CompilerParams(dimension_semantics=("arbitrary",)),
    )(coords, live_counts, tiles, orig_all, dest_all)
    return out.reshape(step_count, state_width)


def local(
    tiles,
    coords,
    counts,
    anchor_factor,
    dest_factor,
    filter_trans,
    filter_gain,
    transition,
    smooth_gain,
):
    state_width = anchor_factor.shape[1]
    orig_all, dest_all = in_one_piece((anchor_factor, dest_factor), ("tm", "od"), 0, 1)
    partial_value = mttkrp(tiles, coords, counts[:, 0], orig_all, dest_all)
    zero_state = jnp.zeros((state_width,), jnp.float32)
    observed = over_copies(partial_value, "od")
    row_count = observed.shape[0]
    drive = product(observed, filter_gain.T)
    zero_run = run_rows(zero_state, drive, filter_trans, False)
    start_state = forward_start(matrix_power(filter_trans, row_count), zero_run[-1])
    filtered = run_rows(start_state, drive, filter_trans, False)
    last_device = lax.axis_index("tm") == lax.axis_size("tm") - 1
    back_terms = backward_terms(filtered, transition, smooth_gain, last_device)
    zero_back = run_rows(zero_state, back_terms, smooth_gain, True)
    end_state = backward_start(matrix_power(smooth_gain, row_count), zero_back[0])
    smoothed = run_rows(end_state, back_terms, smooth_gain, True)
    return (filtered, smoothed)


def solution(mesh):
    return jax.shard_map(
        local,
        mesh=mesh,
        in_specs=(
            P("tm", "od", None, None),
            P(None, "tm", "od"),
            P("tm", "od"),
            P(("tm", "od"), None),
            P(("tm", "od"), None),
            P(),
            P(),
            P(),
            P(),
        ),
        out_specs=(P("tm", None), P("tm", None)),
        check_vma=False,
    )
```

```python
import jax
import jax.numpy as jnp
from jax import lax
from jax.sharding import PartitionSpec as P
from jax.experimental import pallas as pl
from jax.experimental.pallas import tpu as pltpu

HIGHEST = lax.Precision.HIGHEST


def joined_along(pieces, dim):
    shape = list(pieces.shape[1:])
    shape[dim] *= pieces.shape[0]
    return jnp.moveaxis(pieces, 0, dim).reshape(shape)


def from_everyone(array, axis):
    size = lax.axis_size(axis)
    return lax.all_to_all(
        jnp.broadcast_to(array[None], (size, *array.shape)), axis, 0, 0, tiled=True
    )


def collect(array, axis, dim):
    return joined_along(from_everyone(array, axis), dim)


def in_one_piece(arrays, axis, dim, along):
    widths = [a.shape[along] for a in arrays]
    both = jnp.concatenate(arrays, axis=along)
    filled = lax.all_gather(both, axis, axis=dim, tiled=True)
    return tuple(jnp.split(filled, [sum(widths[:k]) for k in range(1, len(widths))], axis=along))


def over_copies(array, axis):
    everything = from_everyone(array, axis)
    return jnp.sum(everything, axis=0)


def product(left_mat, right_mat):
    return jnp.dot(left_mat, right_mat, precision=HIGHEST)


def matrix_power(matrix, exponent):
    result = None
    squared = matrix
    while exponent > 0:
        if exponent % 2 == 1:
            result = squared
        exponent = exponent // 2
        if exponent > 0:
            squared = product(squared, squared)
    return result


def run_rows(start_state, drive, matrix, reverse):

    def advance(carried, drive_row):
        updated = jnp.dot(matrix, carried, precision=HIGHEST) + drive_row
        return (updated, updated)

    return lax.scan(advance, start_state, drive, reverse=reverse)[1]


def backward_terms(filtered, transition, smooth_gain, last_device):
    predicted = product(filtered, transition.T)
    back_terms = filtered - product(predicted, smooth_gain.T)
    row_ids = lax.broadcasted_iota(jnp.int32, back_terms.shape, 0)
    final_row = jnp.logical_and(last_device, row_ids == back_terms.shape[0] - 1)
    return jnp.where(final_row, filtered, back_terms)


def forward_start(stride, last_state):
    states = collect(last_state[None], "tm", 0)
    own_index = lax.axis_index("tm")

    def forward_horner_step(position, running):
        stepped = jnp.dot(stride, running, precision=HIGHEST) + states[position]
        return jnp.where(position < own_index, stepped, running)

    return lax.fori_loop(0, lax.axis_size("tm"), forward_horner_step, jnp.zeros_like(last_state))


def backward_start(stride, first_state):
    states = collect(first_state[None], "tm", 0)
    own_index = lax.axis_index("tm")
    group_size = lax.axis_size("tm")

    def backward_horner_step(turn, running):
        position = group_size - 1 - turn
        stepped = jnp.dot(stride, running, precision=HIGHEST) + states[position]
        return jnp.where(position > own_index, stepped, running)

    return lax.fori_loop(0, group_size, backward_horner_step, jnp.zeros_like(first_state))


GROUP = 4


def mttkrp_kernel(coords_ref, counts_ref, tiles_ref, table_ref, out_ref):
    step = pl.program_id(0)
    slot_total = tiles_ref.shape[1]
    tile_side = tiles_ref.shape[2]
    state_width = table_ref.shape[1] // 2
    tile_top = table_ref.shape[0] // tile_side - 1
    live = jnp.clip(counts_ref[step], 0, slot_total)

    def slot_term(slot):
        orig_id = jnp.clip(coords_ref[0, step, slot], 0, tile_top)
        dest_id = jnp.clip(coords_ref[1, step, slot], 0, tile_top)
        dest_start = pl.multiple_of(dest_id * tile_side, tile_side)
        orig_start = pl.multiple_of(orig_id * tile_side, tile_side)
        dest_rows = table_ref[pl.ds(dest_start, tile_side), pl.ds(state_width, state_width)]
        orig_rows = table_ref[pl.ds(orig_start, tile_side), pl.ds(0, state_width)]
        tile_dest = jnp.dot(tiles_ref[0, slot], dest_rows, preferred_element_type=jnp.float32)
        return tile_dest * orig_rows.astype(jnp.float32)

    def one_group(group, acc):
        first = group * GROUP
        terms = [slot_term(first + k) for k in range(GROUP)]
        for term in terms:
            acc = acc + term
        return acc

    def one_slot(slot, acc):
        return acc + slot_term(slot)

    full_groups = live // GROUP
    acc = lax.fori_loop(
        0, full_groups, one_group, jnp.zeros((tile_side, state_width), jnp.float32)
    )
    acc = lax.fori_loop(full_groups * GROUP, live, one_slot, acc)
    out_ref[0] = jnp.sum(acc, axis=0, keepdims=True)


def mttkrp(tiles, coords, live_counts, table):
    step_count, slot_count, tile_side, _ = tiles.shape
    state_width = table.shape[1] // 2
    grid_spec = pltpu.PrefetchScalarGridSpec(
        num_scalar_prefetch=2,
        grid=(step_count,),
        in_specs=[
            pl.BlockSpec((1, slot_count, tile_side, tile_side), lambda t, c, n: (t, 0, 0, 0)),
            pl.BlockSpec(table.shape, lambda t, c, n: (0, 0)),
        ],
        out_specs=pl.BlockSpec((1, 1, state_width), lambda t, c, n: (t, 0, 0)),
    )
    out = pl.pallas_call(
        mttkrp_kernel,
        grid_spec=grid_spec,
        out_shape=jax.ShapeDtypeStruct((step_count, 1, state_width), jnp.float32),
        compiler_params=pltpu.CompilerParams(dimension_semantics=("arbitrary",)),
    )(coords, live_counts, tiles, table)
    return out.reshape(step_count, state_width)


def local(
    tiles,
    coords,
    counts,
    anchor_factor,
    dest_factor,
    filter_trans,
    filter_gain,
    transition,
    smooth_gain,
):
    state_width = anchor_factor.shape[1]
    table = lax.all_gather(
        jnp.concatenate((anchor_factor, dest_factor), axis=1), ("tm", "od"), axis=0, tiled=True
    )
    partial_value = mttkrp(tiles, coords, counts[:, 0], table)
    zero_state = jnp.zeros((state_width,), jnp.float32)
    observed = over_copies(partial_value, "od")
    row_count = observed.shape[0]
    drive = product(observed, filter_gain.T)
    zero_run = run_rows(zero_state, drive, filter_trans, False)
    start_state = forward_start(matrix_power(filter_trans, row_count), zero_run[-1])
    filtered = run_rows(start_state, drive, filter_trans, False)
    last_device = lax.axis_index("tm") == lax.axis_size("tm") - 1
    back_terms = backward_terms(filtered, transition, smooth_gain, last_device)
    zero_back = run_rows(zero_state, back_terms, smooth_gain, True)
    end_state = backward_start(matrix_power(smooth_gain, row_count), zero_back[0])
    smoothed = run_rows(end_state, back_terms, smooth_gain, True)
    return (filtered, smoothed)


def solution(mesh):
    return jax.shard_map(
        local,
        mesh=mesh,
        in_specs=(
            P("tm", "od", None, None),
            P(None, "tm", "od"),
            P("tm", "od"),
            P(("tm", "od"), None),
            P(("tm", "od"), None),
            P(),
            P(),
            P(),
            P(),
        ),
        out_specs=(P("tm", None), P("tm", None)),
        check_vma=False,
    )
```

```python
import jax
import jax.numpy as jnp
from jax import lax
from jax.sharding import PartitionSpec as P
from jax.experimental import pallas as pl
from jax.experimental.pallas import tpu as pltpu

HIGHEST = lax.Precision.HIGHEST


def joined_along(pieces, dim):
    shape = list(pieces.shape[1:])
    shape[dim] *= pieces.shape[0]
    return jnp.moveaxis(pieces, 0, dim).reshape(shape)


def from_everyone(array, axis):
    size = lax.axis_size(axis)
    return lax.all_to_all(
        jnp.broadcast_to(array[None], (size, *array.shape)), axis, 0, 0, tiled=True
    )


def collect(array, axis, dim):
    return joined_along(from_everyone(array, axis), dim)


def in_one_piece(arrays, axis, dim, along):
    widths = [a.shape[along] for a in arrays]
    both = jnp.concatenate(arrays, axis=along)
    filled = lax.all_gather(both, axis, axis=dim, tiled=True)
    return tuple(jnp.split(filled, [sum(widths[:k]) for k in range(1, len(widths))], axis=along))


def over_copies(array, axis):
    everything = from_everyone(array, axis)
    return jnp.sum(everything, axis=0)


def product(left_mat, right_mat):
    return jnp.dot(left_mat, right_mat, precision=HIGHEST)


def matrix_power(matrix, exponent):
    result = None
    squared = matrix
    while exponent > 0:
        if exponent % 2 == 1:
            result = squared
        exponent = exponent // 2
        if exponent > 0:
            squared = product(squared, squared)
    return result


def run_rows(start_state, drive, matrix, reverse):

    def advance(carried, drive_row):
        updated = jnp.dot(matrix, carried, precision=HIGHEST) + drive_row
        return (updated, updated)

    return lax.scan(advance, start_state, drive, reverse=reverse)[1]


def backward_terms(filtered, transition, smooth_gain, last_device):
    predicted = product(filtered, transition.T)
    back_terms = filtered - product(predicted, smooth_gain.T)
    row_ids = lax.broadcasted_iota(jnp.int32, back_terms.shape, 0)
    final_row = jnp.logical_and(last_device, row_ids == back_terms.shape[0] - 1)
    return jnp.where(final_row, filtered, back_terms)


def forward_start(stride, last_state):
    states = collect(last_state[None], "tm", 0)
    own_index = lax.axis_index("tm")

    def forward_horner_step(position, running):
        stepped = jnp.dot(stride, running, precision=HIGHEST) + states[position]
        return jnp.where(position < own_index, stepped, running)

    return lax.fori_loop(0, lax.axis_size("tm"), forward_horner_step, jnp.zeros_like(last_state))


def backward_start(stride, first_state):
    states = collect(first_state[None], "tm", 0)
    own_index = lax.axis_index("tm")
    group_size = lax.axis_size("tm")

    def backward_horner_step(turn, running):
        position = group_size - 1 - turn
        stepped = jnp.dot(stride, running, precision=HIGHEST) + states[position]
        return jnp.where(position > own_index, stepped, running)

    return lax.fori_loop(0, group_size, backward_horner_step, jnp.zeros_like(first_state))


def powers_of(matrix, top):
    eye = jnp.eye(matrix.shape[0], dtype=matrix.dtype)
    found = [eye, matrix]
    while len(found) <= top:
        reached = found[-1]
        more = jnp.einsum("ij,bjk->bik", reached, jnp.stack(found[1:]), precision=HIGHEST)
        found.extend(list(more))
    return jnp.stack(found[: top + 1])


def forward_sum(spread):
    rows = spread.shape[0]
    total = spread[:, 0]
    for lag in range(1, rows):
        total = total + jnp.pad(spread[: rows - lag, lag], ((lag, 0), (0, 0)))
    return total


def backward_sum(spread):
    rows = spread.shape[0]
    total = spread[:, 0]
    for lag in range(1, rows):
        total = total + jnp.pad(spread[lag:, lag], ((0, lag), (0, 0)))
    return total


def by_powers(rows_in, power_stack):
    return jnp.einsum("kr,jsr->kjs", rows_in, power_stack, precision=HIGHEST)


def kalman(partial_value, filter_trans, filter_gain, transition, smooth_gain):
    rows, width = partial_value.shape
    block = lax.axis_index("tm")
    blocks = lax.axis_size("tm")
    last_device = block == blocks - 1
    filter_powers = powers_of(filter_trans, rows)
    smooth_powers = powers_of(smooth_gain, rows)
    filter_strides = powers_of(filter_powers[rows], blocks - 1)
    smooth_strides = powers_of(smooth_powers[rows], blocks - 1)
    eye = jnp.eye(width, dtype=jnp.float32)
    correction = eye - product(smooth_gain, transition)
    carried = jnp.einsum(
        "tij,tjk->tik",
        smooth_powers[:rows],
        jnp.einsum("ij,tjk->tik", correction, filter_powers[1:], precision=HIGHEST),
        precision=HIGHEST,
    )
    lead_map = jnp.sum(carried, axis=0)
    tail_fix = product(smooth_powers[rows - 1], product(eye - correction, filter_powers[rows]))
    last_map = lead_map + tail_fix

    observed = over_copies(partial_value, "od")
    drive = product(observed, filter_gain.T)
    zero_run = forward_sum(by_powers(drive, filter_powers[:rows]))
    zero_back = backward_terms(zero_run, transition, smooth_gain, last_device)
    zero_smooth = backward_sum(by_powers(zero_back, smooth_powers[:rows]))
    ends = collect(jnp.concatenate((zero_run[rows - 1], zero_smooth[0]))[None], "tm", 0)
    filter_ends = ends[:, :width]
    smooth_starts = ends[:, width:]

    stride_ids = lax.broadcasted_iota(jnp.int32, (blocks, blocks, blocks), 1)
    source_ids = lax.broadcasted_iota(jnp.int32, (blocks, blocks, blocks), 2)
    target_ids = lax.broadcasted_iota(jnp.int32, (blocks, blocks, blocks), 0)
    pick = (stride_ids == target_ids - 1 - source_ids).astype(jnp.float32)
    spread_ends = jnp.einsum("msr,kr->mks", filter_strides, filter_ends, precision=HIGHEST)
    starts = jnp.einsum("bmk,mks->bs", pick, spread_ends, precision=HIGHEST)
    block_ids = lax.broadcasted_iota(jnp.int32, (blocks, width), 0)
    through = jnp.where(
        block_ids == blocks - 1, product(starts, last_map.T), product(starts, lead_map.T)
    )
    smooth_full = smooth_starts + through
    spread_starts = jnp.einsum("msr,kr->mks", smooth_strides, smooth_full, precision=HIGHEST)
    mk_stride = lax.broadcasted_iota(jnp.int32, (blocks, blocks), 0)
    mk_source = lax.broadcasted_iota(jnp.int32, (blocks, blocks), 1)
    later_pick = (mk_stride == mk_source - block - 1).astype(jnp.float32)
    end_state = jnp.einsum("mk,mks->s", later_pick, spread_starts, precision=HIGHEST)
    own_pick = (lax.broadcasted_iota(jnp.int32, (blocks,), 0) == block).astype(jnp.float32)
    start_state = jnp.einsum("b,bs->s", own_pick, starts, precision=HIGHEST)

    filtered = zero_run + jnp.einsum("jsr,r->js", filter_powers[1:], start_state, precision=HIGHEST)
    back_terms = backward_terms(filtered, transition, smooth_gain, last_device)
    local_smooth = backward_sum(by_powers(back_terms, smooth_powers[:rows]))
    smoothed = local_smooth + jnp.einsum(
        "jsr,r->js", smooth_powers[rows:0:-1], end_state, precision=HIGHEST
    )
    return filtered, smoothed


GROUP = 4


def mttkrp_kernel(coords_ref, counts_ref, tiles_ref, table_ref, out_ref):
    step = pl.program_id(0)
    slot_total = tiles_ref.shape[1]
    tile_side = tiles_ref.shape[2]
    state_width = table_ref.shape[1] // 2
    tile_top = table_ref.shape[0] // tile_side - 1
    live = jnp.clip(counts_ref[step], 0, slot_total)

    def slot_term(slot):
        orig_id = jnp.clip(coords_ref[0, step, slot], 0, tile_top)
        dest_id = jnp.clip(coords_ref[1, step, slot], 0, tile_top)
        dest_start = pl.multiple_of(dest_id * tile_side, tile_side)
        orig_start = pl.multiple_of(orig_id * tile_side, tile_side)
        dest_rows = table_ref[pl.ds(dest_start, tile_side), pl.ds(state_width, state_width)]
        orig_rows = table_ref[pl.ds(orig_start, tile_side), pl.ds(0, state_width)]
        tile_dest = jnp.dot(tiles_ref[0, slot], dest_rows, preferred_element_type=jnp.float32)
        return tile_dest * orig_rows.astype(jnp.float32)

    def one_group(group, acc):
        first = group * GROUP
        terms = [slot_term(first + k) for k in range(GROUP)]
        for term in terms:
            acc = acc + term
        return acc

    def one_slot(slot, acc):
        return acc + slot_term(slot)

    full_groups = live // GROUP
    acc = lax.fori_loop(
        0, full_groups, one_group, jnp.zeros((tile_side, state_width), jnp.float32)
    )
    acc = lax.fori_loop(full_groups * GROUP, live, one_slot, acc)
    out_ref[0] = jnp.sum(acc, axis=0, keepdims=True)


def mttkrp(tiles, coords, live_counts, table):
    step_count, slot_count, tile_side, _ = tiles.shape
    state_width = table.shape[1] // 2
    grid_spec = pltpu.PrefetchScalarGridSpec(
        num_scalar_prefetch=2,
        grid=(step_count,),
        in_specs=[
            pl.BlockSpec((1, slot_count, tile_side, tile_side), lambda t, c, n: (t, 0, 0, 0)),
            pl.BlockSpec(table.shape, lambda t, c, n: (0, 0)),
        ],
        out_specs=pl.BlockSpec((1, 1, state_width), lambda t, c, n: (t, 0, 0)),
    )
    out = pl.pallas_call(
        mttkrp_kernel,
        grid_spec=grid_spec,
        out_shape=jax.ShapeDtypeStruct((step_count, 1, state_width), jnp.float32),
        compiler_params=pltpu.CompilerParams(dimension_semantics=("arbitrary",)),
    )(coords, live_counts, tiles, table)
    return out.reshape(step_count, state_width)


def local(
    tiles,
    coords,
    counts,
    anchor_factor,
    dest_factor,
    filter_trans,
    filter_gain,
    transition,
    smooth_gain,
):
    state_width = anchor_factor.shape[1]
    table = lax.all_gather(
        jnp.concatenate((anchor_factor, dest_factor), axis=1), ("tm", "od"), axis=0, tiled=True
    )
    partial_value = mttkrp(tiles, coords, counts[:, 0], table)
    return kalman(partial_value, filter_trans, filter_gain, transition, smooth_gain)


def solution(mesh):
    return jax.shard_map(
        local,
        mesh=mesh,
        in_specs=(
            P("tm", "od", None, None),
            P(None, "tm", "od"),
            P("tm", "od"),
            P(("tm", "od"), None),
            P(("tm", "od"), None),
            P(),
            P(),
            P(),
            P(),
        ),
        out_specs=(P("tm", None), P("tm", None)),
        check_vma=False,
    )
```

```python
import jax
import jax.numpy as jnp
from jax import lax
from jax.sharding import PartitionSpec as P
from jax.experimental import pallas as pl
from jax.experimental.pallas import tpu as pltpu

HIGHEST = lax.Precision.HIGHEST


def joined_along(pieces, dim):
    shape = list(pieces.shape[1:])
    shape[dim] *= pieces.shape[0]
    return jnp.moveaxis(pieces, 0, dim).reshape(shape)


def from_everyone(array, axis):
    size = lax.axis_size(axis)
    return lax.all_to_all(
        jnp.broadcast_to(array[None], (size, *array.shape)), axis, 0, 0, tiled=True
    )


def collect(array, axis, dim):
    return joined_along(from_everyone(array, axis), dim)


def in_one_piece(arrays, axis, dim, along):
    widths = [a.shape[along] for a in arrays]
    both = jnp.concatenate(arrays, axis=along)
    filled = lax.all_gather(both, axis, axis=dim, tiled=True)
    return tuple(jnp.split(filled, [sum(widths[:k]) for k in range(1, len(widths))], axis=along))


def over_copies(array, axis):
    everything = from_everyone(array, axis)
    return jnp.sum(everything, axis=0)


def product(left_mat, right_mat):
    return jnp.dot(left_mat, right_mat, precision=HIGHEST)


def matrix_power(matrix, exponent):
    result = None
    squared = matrix
    while exponent > 0:
        if exponent % 2 == 1:
            result = squared
        exponent = exponent // 2
        if exponent > 0:
            squared = product(squared, squared)
    return result


def run_rows(start_state, drive, matrix, reverse):

    def advance(carried, drive_row):
        updated = jnp.dot(matrix, carried, precision=HIGHEST) + drive_row
        return (updated, updated)

    return lax.scan(advance, start_state, drive, reverse=reverse)[1]


def backward_terms(filtered, transition, smooth_gain, last_device):
    predicted = product(filtered, transition.T)
    back_terms = filtered - product(predicted, smooth_gain.T)
    row_ids = lax.broadcasted_iota(jnp.int32, back_terms.shape, 0)
    final_row = jnp.logical_and(last_device, row_ids == back_terms.shape[0] - 1)
    return jnp.where(final_row, filtered, back_terms)


def forward_start(stride, last_state):
    states = collect(last_state[None], "tm", 0)
    own_index = lax.axis_index("tm")

    def forward_horner_step(position, running):
        stepped = jnp.dot(stride, running, precision=HIGHEST) + states[position]
        return jnp.where(position < own_index, stepped, running)

    return lax.fori_loop(0, lax.axis_size("tm"), forward_horner_step, jnp.zeros_like(last_state))


def backward_start(stride, first_state):
    states = collect(first_state[None], "tm", 0)
    own_index = lax.axis_index("tm")
    group_size = lax.axis_size("tm")

    def backward_horner_step(turn, running):
        position = group_size - 1 - turn
        stepped = jnp.dot(stride, running, precision=HIGHEST) + states[position]
        return jnp.where(position > own_index, stepped, running)

    return lax.fori_loop(0, group_size, backward_horner_step, jnp.zeros_like(first_state))


def powers_of(matrices, top):
    eye = jnp.broadcast_to(jnp.eye(matrices.shape[1], dtype=matrices.dtype), matrices.shape)
    found = [eye, matrices]
    while len(found) <= top:
        reached = found[-1]
        more = jnp.einsum("pij,bpjk->bpik", reached, jnp.stack(found[1:]), precision=HIGHEST)
        found.extend(list(more))
    return jnp.stack(found[: top + 1])


def shift_pick(rows, later):
    out_ids = lax.broadcasted_iota(jnp.int32, (rows, rows, rows), 0)
    in_ids = lax.broadcasted_iota(jnp.int32, (rows, rows, rows), 1)
    lag_ids = lax.broadcasted_iota(jnp.int32, (rows, rows, rows), 2)
    source = out_ids + lag_ids if later else out_ids - lag_ids
    return (in_ids == source).astype(jnp.float32)


def forward_sum(spread):
    pick = shift_pick(spread.shape[0], False)
    return jnp.einsum("tkj,kjs->ts", pick, spread, precision=HIGHEST)


def backward_sum(spread):
    pick = shift_pick(spread.shape[0], True)
    return jnp.einsum("tkj,kjs->ts", pick, spread, precision=HIGHEST)


def by_powers(rows_in, power_stack):
    return jnp.einsum("kr,jsr->kjs", rows_in, power_stack, precision=HIGHEST)


def kalman(partial_value, filter_trans, filter_gain, transition, smooth_gain):
    rows, width = partial_value.shape
    block = lax.axis_index("tm")
    blocks = lax.axis_size("tm")
    last_device = block == blocks - 1
    both_powers = powers_of(jnp.stack((filter_trans, smooth_gain)), rows)
    filter_powers = both_powers[:, 0]
    smooth_powers = both_powers[:, 1]
    both_strides = powers_of(both_powers[rows], blocks - 1)
    filter_strides = both_strides[:, 0]
    smooth_strides = both_strides[:, 1]
    eye = jnp.eye(width, dtype=jnp.float32)
    correction = eye - product(smooth_gain, transition)
    carried = jnp.einsum(
        "tij,tjk->tik",
        smooth_powers[:rows],
        jnp.einsum("ij,tjk->tik", correction, filter_powers[1:], precision=HIGHEST),
        precision=HIGHEST,
    )
    lead_map = jnp.sum(carried, axis=0)
    tail_fix = product(smooth_powers[rows - 1], product(eye - correction, filter_powers[rows]))
    last_map = lead_map + tail_fix

    observed = over_copies(partial_value, "od")
    drive = product(observed, filter_gain.T)
    zero_run = forward_sum(by_powers(drive, filter_powers[:rows]))
    zero_back = backward_terms(zero_run, transition, smooth_gain, last_device)
    zero_smooth = backward_sum(by_powers(zero_back, smooth_powers[:rows]))
    ends = collect(jnp.concatenate((zero_run[rows - 1], zero_smooth[0]))[None], "tm", 0)
    filter_ends = ends[:, :width]
    smooth_starts = ends[:, width:]

    stride_ids = lax.broadcasted_iota(jnp.int32, (blocks, blocks, blocks), 1)
    source_ids = lax.broadcasted_iota(jnp.int32, (blocks, blocks, blocks), 2)
    target_ids = lax.broadcasted_iota(jnp.int32, (blocks, blocks, blocks), 0)
    pick = (stride_ids == target_ids - 1 - source_ids).astype(jnp.float32)
    spread_ends = jnp.einsum("msr,kr->mks", filter_strides, filter_ends, precision=HIGHEST)
    starts = jnp.einsum("bmk,mks->bs", pick, spread_ends, precision=HIGHEST)
    block_ids = lax.broadcasted_iota(jnp.int32, (blocks, width), 0)
    through = jnp.where(
        block_ids == blocks - 1, product(starts, last_map.T), product(starts, lead_map.T)
    )
    smooth_full = smooth_starts + through
    spread_starts = jnp.einsum("msr,kr->mks", smooth_strides, smooth_full, precision=HIGHEST)
    mk_stride = lax.broadcasted_iota(jnp.int32, (blocks, blocks), 0)
    mk_source = lax.broadcasted_iota(jnp.int32, (blocks, blocks), 1)
    later_pick = (mk_stride == mk_source - block - 1).astype(jnp.float32)
    end_state = jnp.einsum("mk,mks->s", later_pick, spread_starts, precision=HIGHEST)
    own_pick = (lax.broadcasted_iota(jnp.int32, (blocks,), 0) == block).astype(jnp.float32)
    start_state = jnp.einsum("b,bs->s", own_pick, starts, precision=HIGHEST)

    filtered = zero_run + jnp.einsum("jsr,r->js", filter_powers[1:], start_state, precision=HIGHEST)
    back_terms = backward_terms(filtered, transition, smooth_gain, last_device)
    local_smooth = backward_sum(by_powers(back_terms, smooth_powers[:rows]))
    carried_end = jnp.einsum("jsr,r->js", smooth_powers[1:], end_state, precision=HIGHEST)
    smoothed = local_smooth + jnp.flip(carried_end, axis=0)
    return filtered, smoothed


GROUP = 4


def mttkrp_kernel(coords_ref, counts_ref, tiles_ref, table_ref, out_ref, orig_ref):
    step = pl.program_id(0)
    slot_total = tiles_ref.shape[1]
    tile_side = tiles_ref.shape[2]
    state_width = orig_ref.shape[1]
    tile_top = table_ref.shape[0] // tile_side - 1

    @pl.when(step == 0)
    def _():
        orig_ref[...] = table_ref[:, pl.ds(0, state_width)].astype(jnp.float32)

    live = jnp.clip(counts_ref[step], 0, slot_total)

    def slot_term(slot):
        orig_id = jnp.clip(coords_ref[0, step, slot], 0, tile_top)
        dest_id = jnp.clip(coords_ref[1, step, slot], 0, tile_top)
        dest_start = pl.multiple_of(dest_id * tile_side, tile_side)
        orig_start = pl.multiple_of(orig_id * tile_side, tile_side)
        dest_rows = table_ref[pl.ds(dest_start, tile_side), pl.ds(state_width, state_width)]
        orig_rows = orig_ref[pl.ds(orig_start, tile_side), :]
        tile_dest = jnp.dot(tiles_ref[0, slot], dest_rows, preferred_element_type=jnp.float32)
        weighted = tile_dest * orig_rows
        return jnp.sum(weighted.reshape(tile_side // 8, 8, state_width), axis=0)

    def one_group(group, acc):
        first = group * GROUP
        terms = [slot_term(first + k) for k in range(GROUP)]
        return acc + ((terms[0] + terms[1]) + (terms[2] + terms[3]))

    def one_slot(slot, acc):
        return acc + slot_term(slot)

    full_groups = live // GROUP
    acc = lax.fori_loop(0, full_groups, one_group, jnp.zeros((8, state_width), jnp.float32))
    acc = lax.fori_loop(full_groups * GROUP, live, one_slot, acc)
    out_ref[0] = jnp.sum(acc, axis=0, keepdims=True)


def mttkrp(tiles, coords, live_counts, table):
    step_count, slot_count, tile_side, _ = tiles.shape
    state_width = table.shape[1] // 2
    grid_spec = pltpu.PrefetchScalarGridSpec(
        num_scalar_prefetch=2,
        grid=(step_count,),
        in_specs=[
            pl.BlockSpec((1, slot_count, tile_side, tile_side), lambda t, c, n: (t, 0, 0, 0)),
            pl.BlockSpec(table.shape, lambda t, c, n: (0, 0)),
        ],
        out_specs=pl.BlockSpec((1, 1, state_width), lambda t, c, n: (t, 0, 0)),
        scratch_shapes=[pltpu.VMEM((table.shape[0], state_width), jnp.float32)],
    )
    out = pl.pallas_call(
        mttkrp_kernel,
        grid_spec=grid_spec,
        out_shape=jax.ShapeDtypeStruct((step_count, 1, state_width), jnp.float32),
        compiler_params=pltpu.CompilerParams(dimension_semantics=("arbitrary",)),
    )(coords, live_counts, tiles, table)
    return out.reshape(step_count, state_width)


def local(
    tiles,
    coords,
    counts,
    anchor_factor,
    dest_factor,
    filter_trans,
    filter_gain,
    transition,
    smooth_gain,
):
    state_width = anchor_factor.shape[1]
    table = lax.all_gather(
        jnp.concatenate((anchor_factor, dest_factor), axis=1), ("tm", "od"), axis=0, tiled=True
    )
    partial_value = mttkrp(tiles, coords, counts[:, 0], table)
    return kalman(partial_value, filter_trans, filter_gain, transition, smooth_gain)


def solution(mesh):
    return jax.shard_map(
        local,
        mesh=mesh,
        in_specs=(
            P("tm", "od", None, None),
            P(None, "tm", "od"),
            P("tm", "od"),
            P(("tm", "od"), None),
            P(("tm", "od"), None),
            P(),
            P(),
            P(),
            P(),
        ),
        out_specs=(P("tm", None), P("tm", None)),
        check_vma=False,
    )
```

```python
import jax
import jax.numpy as jnp
from jax import lax
from jax.sharding import PartitionSpec as P
from jax.experimental import pallas as pl
from jax.experimental.pallas import tpu as pltpu

HIGHEST = lax.Precision.HIGHEST


def joined_along(pieces, dim):
    shape = list(pieces.shape[1:])
    shape[dim] *= pieces.shape[0]
    return jnp.moveaxis(pieces, 0, dim).reshape(shape)


def from_everyone(array, axis):
    size = lax.axis_size(axis)
    return lax.all_to_all(
        jnp.broadcast_to(array[None], (size, *array.shape)), axis, 0, 0, tiled=True
    )


def collect(array, axis, dim):
    return joined_along(from_everyone(array, axis), dim)


def in_one_piece(arrays, axis, dim, along):
    widths = [a.shape[along] for a in arrays]
    both = jnp.concatenate(arrays, axis=along)
    filled = lax.all_gather(both, axis, axis=dim, tiled=True)
    return tuple(jnp.split(filled, [sum(widths[:k]) for k in range(1, len(widths))], axis=along))


def over_copies(array, axis):
    everything = from_everyone(array, axis)
    return jnp.sum(everything, axis=0)


def product(left_mat, right_mat):
    return jnp.dot(left_mat, right_mat, precision=HIGHEST)


def matrix_power(matrix, exponent):
    result = None
    squared = matrix
    while exponent > 0:
        if exponent % 2 == 1:
            result = squared
        exponent = exponent // 2
        if exponent > 0:
            squared = product(squared, squared)
    return result


def run_rows(start_state, drive, matrix, reverse):

    def advance(carried, drive_row):
        updated = jnp.dot(matrix, carried, precision=HIGHEST) + drive_row
        return (updated, updated)

    return lax.scan(advance, start_state, drive, reverse=reverse)[1]


def backward_terms(filtered, transition, smooth_gain, last_device):
    predicted = product(filtered, transition.T)
    back_terms = filtered - product(predicted, smooth_gain.T)
    row_ids = lax.broadcasted_iota(jnp.int32, back_terms.shape, 0)
    final_row = jnp.logical_and(last_device, row_ids == back_terms.shape[0] - 1)
    return jnp.where(final_row, filtered, back_terms)


def forward_start(stride, last_state):
    states = collect(last_state[None], "tm", 0)
    own_index = lax.axis_index("tm")

    def forward_horner_step(position, running):
        stepped = jnp.dot(stride, running, precision=HIGHEST) + states[position]
        return jnp.where(position < own_index, stepped, running)

    return lax.fori_loop(0, lax.axis_size("tm"), forward_horner_step, jnp.zeros_like(last_state))


def backward_start(stride, first_state):
    states = collect(first_state[None], "tm", 0)
    own_index = lax.axis_index("tm")
    group_size = lax.axis_size("tm")

    def backward_horner_step(turn, running):
        position = group_size - 1 - turn
        stepped = jnp.dot(stride, running, precision=HIGHEST) + states[position]
        return jnp.where(position > own_index, stepped, running)

    return lax.fori_loop(0, group_size, backward_horner_step, jnp.zeros_like(first_state))


def powers_of(matrices, top):
    eye = jnp.broadcast_to(jnp.eye(matrices.shape[1], dtype=matrices.dtype), matrices.shape)
    found = [eye, matrices]
    while len(found) <= top:
        reached = found[-1]
        more = jnp.einsum("pij,bpjk->bpik", reached, jnp.stack(found[1:]), precision=HIGHEST)
        found.extend(list(more))
    return jnp.stack(found[: top + 1])


def forward_sum(spread):
    rows = spread.shape[0]
    total = spread[:, 0]
    for lag in range(1, rows):
        total = total + jnp.pad(spread[: rows - lag, lag], ((lag, 0), (0, 0)))
    return total


def backward_sum(spread):
    rows = spread.shape[0]
    total = spread[:, 0]
    for lag in range(1, rows):
        total = total + jnp.pad(spread[lag:, lag], ((0, lag), (0, 0)))
    return total


def by_powers(rows_in, power_stack):
    return jnp.einsum("kr,jsr->kjs", rows_in, power_stack, precision=HIGHEST)


def kalman(partial_value, filter_trans, filter_gain, transition, smooth_gain):
    rows, width = partial_value.shape
    block = lax.axis_index("tm")
    blocks = lax.axis_size("tm")
    last_device = block == blocks - 1
    both_powers = powers_of(jnp.stack((filter_trans, smooth_gain)), rows)
    filter_powers = both_powers[:, 0]
    smooth_powers = both_powers[:, 1]
    both_strides = powers_of(both_powers[rows], blocks - 1)
    filter_strides = both_strides[:, 0]
    smooth_strides = both_strides[:, 1]
    eye = jnp.eye(width, dtype=jnp.float32)
    correction = eye - product(smooth_gain, transition)
    carried = jnp.einsum(
        "tij,tjk->tik",
        smooth_powers[:rows],
        jnp.einsum("ij,tjk->tik", correction, filter_powers[1:], precision=HIGHEST),
        precision=HIGHEST,
    )
    lead_map = jnp.sum(carried, axis=0)
    tail_fix = product(smooth_powers[rows - 1], product(eye - correction, filter_powers[rows]))
    last_map = lead_map + tail_fix

    observed = over_copies(partial_value, "od")
    drive = product(observed, filter_gain.T)
    zero_run = forward_sum(by_powers(drive, filter_powers[:rows]))
    zero_back = backward_terms(zero_run, transition, smooth_gain, last_device)
    zero_smooth = backward_sum(by_powers(zero_back, smooth_powers[:rows]))
    ends = collect(jnp.concatenate((zero_run[rows - 1], zero_smooth[0]))[None], "tm", 0)
    filter_ends = ends[:, :width]
    smooth_starts = ends[:, width:]

    stride_ids = lax.broadcasted_iota(jnp.int32, (blocks, blocks, blocks), 1)
    source_ids = lax.broadcasted_iota(jnp.int32, (blocks, blocks, blocks), 2)
    target_ids = lax.broadcasted_iota(jnp.int32, (blocks, blocks, blocks), 0)
    pick = (stride_ids == target_ids - 1 - source_ids).astype(jnp.float32)
    spread_ends = jnp.einsum("msr,kr->mks", filter_strides, filter_ends, precision=HIGHEST)
    starts = jnp.einsum("bmk,mks->bs", pick, spread_ends, precision=HIGHEST)
    block_ids = lax.broadcasted_iota(jnp.int32, (blocks, width), 0)
    through = jnp.where(
        block_ids == blocks - 1, product(starts, last_map.T), product(starts, lead_map.T)
    )
    smooth_full = smooth_starts + through
    spread_starts = jnp.einsum("msr,kr->mks", smooth_strides, smooth_full, precision=HIGHEST)
    mk_stride = lax.broadcasted_iota(jnp.int32, (blocks, blocks), 0)
    mk_source = lax.broadcasted_iota(jnp.int32, (blocks, blocks), 1)
    later_pick = (mk_stride == mk_source - block - 1).astype(jnp.float32)
    end_state = jnp.einsum("mk,mks->s", later_pick, spread_starts, precision=HIGHEST)
    own_pick = (lax.broadcasted_iota(jnp.int32, (blocks,), 0) == block).astype(jnp.float32)
    start_state = jnp.einsum("b,bs->s", own_pick, starts, precision=HIGHEST)

    filtered = zero_run + jnp.einsum("jsr,r->js", filter_powers[1:], start_state, precision=HIGHEST)
    back_terms = backward_terms(filtered, transition, smooth_gain, last_device)
    local_smooth = backward_sum(by_powers(back_terms, smooth_powers[:rows]))
    carried_end = jnp.einsum("jsr,r->js", smooth_powers[1:], end_state, precision=HIGHEST)
    smoothed = local_smooth + jnp.flip(carried_end, axis=0)
    return filtered, smoothed


GROUPS = (16, 4)


def mttkrp_kernel(coords_ref, counts_ref, tiles_ref, table_ref, out_ref, orig_ref):
    step = pl.program_id(0)
    slot_total = tiles_ref.shape[1]
    tile_side = tiles_ref.shape[2]
    state_width = orig_ref.shape[1]
    tile_top = table_ref.shape[0] // tile_side - 1

    @pl.when(step == 0)
    def _():
        orig_ref[...] = table_ref[:, pl.ds(0, state_width)].astype(jnp.float32)

    live = jnp.clip(counts_ref[step], 0, slot_total)

    def slot_term(slot):
        orig_id = jnp.clip(coords_ref[0, step, slot], 0, tile_top)
        dest_id = jnp.clip(coords_ref[1, step, slot], 0, tile_top)
        dest_start = pl.multiple_of(dest_id * tile_side, tile_side)
        orig_start = pl.multiple_of(orig_id * tile_side, tile_side)
        dest_rows = table_ref[pl.ds(dest_start, tile_side), pl.ds(state_width, state_width)]
        orig_rows = orig_ref[pl.ds(orig_start, tile_side), :]
        tile_dest = jnp.dot(tiles_ref[0, slot], dest_rows, preferred_element_type=jnp.float32)
        weighted = tile_dest * orig_rows
        return jnp.sum(weighted.reshape(tile_side // 8, 8, state_width), axis=0)

    def group_of(width, first):
        def one_group(group, acc):
            terms = [slot_term(first + group * width + k) for k in range(width)]
            while len(terms) > 1:
                terms = [terms[k] + terms[k + 1] for k in range(0, len(terms), 2)]
            return acc + terms[0]

        return one_group

    def one_slot(slot, acc):
        return acc + slot_term(slot)

    acc = jnp.zeros((8, state_width), jnp.float32)
    done = 0
    for width in GROUPS:
        groups = (live - done) // width
        acc = lax.fori_loop(0, groups, group_of(width, done), acc)
        done = done + groups * width
    acc = lax.fori_loop(done, live, one_slot, acc)
    out_ref[0] = jnp.sum(acc, axis=0, keepdims=True)


def mttkrp(tiles, coords, live_counts, table):
    step_count, slot_count, tile_side, _ = tiles.shape
    state_width = table.shape[1] // 2
    grid_spec = pltpu.PrefetchScalarGridSpec(
        num_scalar_prefetch=2,
        grid=(step_count,),
        in_specs=[
            pl.BlockSpec((1, slot_count, tile_side, tile_side), lambda t, c, n: (t, 0, 0, 0)),
            pl.BlockSpec(table.shape, lambda t, c, n: (0, 0)),
        ],
        out_specs=pl.BlockSpec((1, 1, state_width), lambda t, c, n: (t, 0, 0)),
        scratch_shapes=[pltpu.VMEM((table.shape[0], state_width), jnp.float32)],
    )
    out = pl.pallas_call(
        mttkrp_kernel,
        grid_spec=grid_spec,
        out_shape=jax.ShapeDtypeStruct((step_count, 1, state_width), jnp.float32),
        compiler_params=pltpu.CompilerParams(dimension_semantics=("arbitrary",)),
    )(coords, live_counts, tiles, table)
    return out.reshape(step_count, state_width)


def local(
    tiles,
    coords,
    counts,
    anchor_factor,
    dest_factor,
    filter_trans,
    filter_gain,
    transition,
    smooth_gain,
):
    state_width = anchor_factor.shape[1]
    table = lax.all_gather(
        jnp.concatenate((anchor_factor, dest_factor), axis=1), ("tm", "od"), axis=0, tiled=True
    )
    partial_value = mttkrp(tiles, coords, counts[:, 0], table)
    return kalman(partial_value, filter_trans, filter_gain, transition, smooth_gain)


def solution(mesh):
    return jax.shard_map(
        local,
        mesh=mesh,
        in_specs=(
            P("tm", "od", None, None),
            P(None, "tm", "od"),
            P("tm", "od"),
            P(("tm", "od"), None),
            P(("tm", "od"), None),
            P(),
            P(),
            P(),
            P(),
        ),
        out_specs=(P("tm", None), P("tm", None)),
        check_vma=False,
    )
```

```python
import jax
import jax.numpy as jnp
from jax import lax
from jax.sharding import PartitionSpec as P
from jax.experimental import pallas as pl
from jax.experimental.pallas import tpu as pltpu

HIGHEST = lax.Precision.HIGHEST
HIGH = lax.Precision.HIGH


def joined_along(pieces, dim):
    shape = list(pieces.shape[1:])
    shape[dim] *= pieces.shape[0]
    return jnp.moveaxis(pieces, 0, dim).reshape(shape)


def from_everyone(array, axis):
    size = lax.axis_size(axis)
    return lax.all_to_all(
        jnp.broadcast_to(array[None], (size, *array.shape)), axis, 0, 0, tiled=True
    )


def collect(array, axis, dim):
    return joined_along(from_everyone(array, axis), dim)


def in_one_piece(arrays, axis, dim, along):
    widths = [a.shape[along] for a in arrays]
    both = jnp.concatenate(arrays, axis=along)
    filled = lax.all_gather(both, axis, axis=dim, tiled=True)
    return tuple(jnp.split(filled, [sum(widths[:k]) for k in range(1, len(widths))], axis=along))


def over_copies(array, axis):
    everything = from_everyone(array, axis)
    return jnp.sum(everything, axis=0)


def product(left_mat, right_mat):
    return jnp.dot(left_mat, right_mat, precision=HIGHEST)


def matrix_power(matrix, exponent):
    result = None
    squared = matrix
    while exponent > 0:
        if exponent % 2 == 1:
            result = squared
        exponent = exponent // 2
        if exponent > 0:
            squared = product(squared, squared)
    return result


def run_rows(start_state, drive, matrix, reverse):

    def advance(carried, drive_row):
        updated = jnp.dot(matrix, carried, precision=HIGHEST) + drive_row
        return (updated, updated)

    return lax.scan(advance, start_state, drive, reverse=reverse)[1]


def backward_terms(filtered, transition, smooth_gain, last_device):
    predicted = product(filtered, transition.T)
    back_terms = filtered - product(predicted, smooth_gain.T)
    row_ids = lax.broadcasted_iota(jnp.int32, back_terms.shape, 0)
    final_row = jnp.logical_and(last_device, row_ids == back_terms.shape[0] - 1)
    return jnp.where(final_row, filtered, back_terms)


def forward_start(stride, last_state):
    states = collect(last_state[None], "tm", 0)
    own_index = lax.axis_index("tm")

    def forward_horner_step(position, running):
        stepped = jnp.dot(stride, running, precision=HIGHEST) + states[position]
        return jnp.where(position < own_index, stepped, running)

    return lax.fori_loop(0, lax.axis_size("tm"), forward_horner_step, jnp.zeros_like(last_state))


def backward_start(stride, first_state):
    states = collect(first_state[None], "tm", 0)
    own_index = lax.axis_index("tm")
    group_size = lax.axis_size("tm")

    def backward_horner_step(turn, running):
        position = group_size - 1 - turn
        stepped = jnp.dot(stride, running, precision=HIGHEST) + states[position]
        return jnp.where(position > own_index, stepped, running)

    return lax.fori_loop(0, group_size, backward_horner_step, jnp.zeros_like(first_state))


def powers_of(matrices, top):
    eye = jnp.broadcast_to(jnp.eye(matrices.shape[1], dtype=matrices.dtype), matrices.shape)
    found = [eye, matrices]
    while len(found) <= top:
        reached = found[-1]
        more = jnp.einsum("pij,bpjk->bpik", reached, jnp.stack(found[1:]), precision=HIGHEST)
        found.extend(list(more))
    return jnp.stack(found[: top + 1])


def forward_sum(spread):
    rows = spread.shape[0]
    total = spread[:, 0]
    for lag in range(1, rows):
        total = total + jnp.pad(spread[: rows - lag, lag], ((lag, 0), (0, 0)))
    return total


def backward_sum(spread):
    rows = spread.shape[0]
    total = spread[:, 0]
    for lag in range(1, rows):
        total = total + jnp.pad(spread[lag:, lag], ((0, lag), (0, 0)))
    return total


def by_powers(rows_in, power_stack):
    return jnp.einsum("kr,jsr->kjs", rows_in, power_stack, precision=HIGH)


def kalman(partial_value, filter_trans, filter_gain, transition, smooth_gain):
    rows, width = partial_value.shape
    block = lax.axis_index("tm")
    blocks = lax.axis_size("tm")
    last_device = block == blocks - 1
    both_powers = powers_of(jnp.stack((filter_trans, smooth_gain)), rows)
    filter_powers = both_powers[:, 0]
    smooth_powers = both_powers[:, 1]
    both_strides = powers_of(both_powers[rows], blocks - 1)
    filter_strides = both_strides[:, 0]
    smooth_strides = both_strides[:, 1]
    eye = jnp.eye(width, dtype=jnp.float32)
    correction = eye - product(smooth_gain, transition)
    carried = jnp.einsum(
        "tij,tjk->tik",
        smooth_powers[:rows],
        jnp.einsum("ij,tjk->tik", correction, filter_powers[1:], precision=HIGHEST),
        precision=HIGHEST,
    )
    lead_map = jnp.sum(carried, axis=0)
    tail_fix = product(smooth_powers[rows - 1], product(eye - correction, filter_powers[rows]))
    last_map = lead_map + tail_fix

    observed = over_copies(partial_value, "od")
    drive = product(observed, filter_gain.T)
    zero_run = forward_sum(by_powers(drive, filter_powers[:rows]))
    zero_back = backward_terms(zero_run, transition, smooth_gain, last_device)
    zero_smooth = backward_sum(by_powers(zero_back, smooth_powers[:rows]))
    ends = collect(jnp.concatenate((zero_run[rows - 1], zero_smooth[0]))[None], "tm", 0)
    filter_ends = ends[:, :width]
    smooth_starts = ends[:, width:]

    stride_ids = lax.broadcasted_iota(jnp.int32, (blocks, blocks, blocks), 1)
    source_ids = lax.broadcasted_iota(jnp.int32, (blocks, blocks, blocks), 2)
    target_ids = lax.broadcasted_iota(jnp.int32, (blocks, blocks, blocks), 0)
    pick = (stride_ids == target_ids - 1 - source_ids).astype(jnp.float32)
    spread_ends = jnp.einsum("msr,kr->mks", filter_strides, filter_ends, precision=HIGH)
    starts = jnp.einsum("bmk,mks->bs", pick, spread_ends, precision=HIGHEST)
    block_ids = lax.broadcasted_iota(jnp.int32, (blocks, width), 0)
    through = jnp.where(
        block_ids == blocks - 1, product(starts, last_map.T), product(starts, lead_map.T)
    )
    smooth_full = smooth_starts + through
    spread_starts = jnp.einsum("msr,kr->mks", smooth_strides, smooth_full, precision=HIGH)
    mk_stride = lax.broadcasted_iota(jnp.int32, (blocks, blocks), 0)
    mk_source = lax.broadcasted_iota(jnp.int32, (blocks, blocks), 1)
    later_pick = (mk_stride == mk_source - block - 1).astype(jnp.float32)
    end_state = jnp.einsum("mk,mks->s", later_pick, spread_starts, precision=HIGHEST)
    own_pick = (lax.broadcasted_iota(jnp.int32, (blocks,), 0) == block).astype(jnp.float32)
    start_state = jnp.einsum("b,bs->s", own_pick, starts, precision=HIGHEST)

    filtered = zero_run + jnp.einsum("jsr,r->js", filter_powers[1:], start_state, precision=HIGH)
    back_terms = backward_terms(filtered, transition, smooth_gain, last_device)
    local_smooth = backward_sum(by_powers(back_terms, smooth_powers[:rows]))
    carried_end = jnp.einsum("jsr,r->js", smooth_powers[1:], end_state, precision=HIGH)
    smoothed = local_smooth + jnp.flip(carried_end, axis=0)
    return filtered, smoothed


GROUPS = (16, 4)


def mttkrp_kernel(coords_ref, counts_ref, tiles_ref, table_ref, out_ref, orig_ref):
    step = pl.program_id(0)
    slot_total = tiles_ref.shape[1]
    tile_side = tiles_ref.shape[2]
    state_width = orig_ref.shape[1]
    tile_top = table_ref.shape[0] // tile_side - 1

    @pl.when(step == 0)
    def _():
        orig_ref[...] = table_ref[:, pl.ds(0, state_width)].astype(jnp.float32)

    live = jnp.clip(counts_ref[step], 0, slot_total)

    def slot_term(slot):
        orig_id = jnp.clip(coords_ref[0, step, slot], 0, tile_top)
        dest_id = jnp.clip(coords_ref[1, step, slot], 0, tile_top)
        dest_start = pl.multiple_of(dest_id * tile_side, tile_side)
        orig_start = pl.multiple_of(orig_id * tile_side, tile_side)
        dest_rows = table_ref[pl.ds(dest_start, tile_side), pl.ds(state_width, state_width)]
        orig_rows = orig_ref[pl.ds(orig_start, tile_side), :]
        tile_dest = jnp.dot(tiles_ref[0, slot], dest_rows, preferred_element_type=jnp.float32)
        weighted = tile_dest * orig_rows
        return jnp.sum(weighted.reshape(tile_side // 8, 8, state_width), axis=0)

    def group_of(width, first):
        def one_group(group, acc):
            terms = [slot_term(first + group * width + k) for k in range(width)]
            while len(terms) > 1:
                terms = [terms[k] + terms[k + 1] for k in range(0, len(terms), 2)]
            return acc + terms[0]

        return one_group

    def one_slot(slot, acc):
        return acc + slot_term(slot)

    acc = jnp.zeros((8, state_width), jnp.float32)
    done = 0
    for width in GROUPS:
        groups = (live - done) // width
        acc = lax.fori_loop(0, groups, group_of(width, done), acc)
        done = done + groups * width
    acc = lax.fori_loop(done, live, one_slot, acc)
    out_ref[0] = jnp.sum(acc, axis=0, keepdims=True)


def mttkrp(tiles, coords, live_counts, table):
    step_count, slot_count, tile_side, _ = tiles.shape
    state_width = table.shape[1] // 2
    grid_spec = pltpu.PrefetchScalarGridSpec(
        num_scalar_prefetch=2,
        grid=(step_count,),
        in_specs=[
            pl.BlockSpec((1, slot_count, tile_side, tile_side), lambda t, c, n: (t, 0, 0, 0)),
            pl.BlockSpec(table.shape, lambda t, c, n: (0, 0)),
        ],
        out_specs=pl.BlockSpec((1, 1, state_width), lambda t, c, n: (t, 0, 0)),
        scratch_shapes=[pltpu.VMEM((table.shape[0], state_width), jnp.float32)],
    )
    out = pl.pallas_call(
        mttkrp_kernel,
        grid_spec=grid_spec,
        out_shape=jax.ShapeDtypeStruct((step_count, 1, state_width), jnp.float32),
        compiler_params=pltpu.CompilerParams(dimension_semantics=("arbitrary",)),
    )(coords, live_counts, tiles, table)
    return out.reshape(step_count, state_width)


def local(
    tiles,
    coords,
    counts,
    anchor_factor,
    dest_factor,
    filter_trans,
    filter_gain,
    transition,
    smooth_gain,
):
    state_width = anchor_factor.shape[1]
    table = collect(jnp.concatenate((anchor_factor, dest_factor), axis=1), ("tm", "od"), 0)
    partial_value = mttkrp(tiles, coords, counts[:, 0], table)
    return kalman(partial_value, filter_trans, filter_gain, transition, smooth_gain)


def solution(mesh):
    return jax.shard_map(
        local,
        mesh=mesh,
        in_specs=(
            P("tm", "od", None, None),
            P(None, "tm", "od"),
            P("tm", "od"),
            P(("tm", "od"), None),
            P(("tm", "od"), None),
            P(),
            P(),
            P(),
            P(),
        ),
        out_specs=(P("tm", None), P("tm", None)),
        check_vma=False,
    )
```

```python
import jax
import jax.numpy as jnp
from jax import lax
from jax.sharding import PartitionSpec as P
from jax.experimental import pallas as pl
from jax.experimental.pallas import tpu as pltpu

HIGHEST = lax.Precision.HIGHEST
HIGH = lax.Precision.HIGH


def joined_along(pieces, dim):
    shape = list(pieces.shape[1:])
    shape[dim] *= pieces.shape[0]
    return jnp.moveaxis(pieces, 0, dim).reshape(shape)


def from_everyone(array, axis):
    size = lax.axis_size(axis)
    return lax.all_to_all(
        jnp.broadcast_to(array[None], (size, *array.shape)), axis, 0, 0, tiled=True
    )


def collect(array, axis, dim):
    return joined_along(from_everyone(array, axis), dim)


def in_one_piece(arrays, axis, dim, along):
    widths = [a.shape[along] for a in arrays]
    both = jnp.concatenate(arrays, axis=along)
    filled = lax.all_gather(both, axis, axis=dim, tiled=True)
    return tuple(jnp.split(filled, [sum(widths[:k]) for k in range(1, len(widths))], axis=along))


def over_copies(array, axis):
    everything = from_everyone(array, axis)
    return jnp.sum(everything, axis=0)


def product(left_mat, right_mat):
    return jnp.dot(left_mat, right_mat, precision=HIGHEST)


def matrix_power(matrix, exponent):
    result = None
    squared = matrix
    while exponent > 0:
        if exponent % 2 == 1:
            result = squared
        exponent = exponent // 2
        if exponent > 0:
            squared = product(squared, squared)
    return result


def run_rows(start_state, drive, matrix, reverse):

    def advance(carried, drive_row):
        updated = jnp.dot(matrix, carried, precision=HIGHEST) + drive_row
        return (updated, updated)

    return lax.scan(advance, start_state, drive, reverse=reverse)[1]


def backward_terms(filtered, transition, smooth_gain, last_device):
    predicted = product(filtered, transition.T)
    back_terms = filtered - product(predicted, smooth_gain.T)
    row_ids = lax.broadcasted_iota(jnp.int32, back_terms.shape, 0)
    final_row = jnp.logical_and(last_device, row_ids == back_terms.shape[0] - 1)
    return jnp.where(final_row, filtered, back_terms)


def forward_start(stride, last_state):
    states = collect(last_state[None], "tm", 0)
    own_index = lax.axis_index("tm")

    def forward_horner_step(position, running):
        stepped = jnp.dot(stride, running, precision=HIGHEST) + states[position]
        return jnp.where(position < own_index, stepped, running)

    return lax.fori_loop(0, lax.axis_size("tm"), forward_horner_step, jnp.zeros_like(last_state))


def backward_start(stride, first_state):
    states = collect(first_state[None], "tm", 0)
    own_index = lax.axis_index("tm")
    group_size = lax.axis_size("tm")

    def backward_horner_step(turn, running):
        position = group_size - 1 - turn
        stepped = jnp.dot(stride, running, precision=HIGHEST) + states[position]
        return jnp.where(position > own_index, stepped, running)

    return lax.fori_loop(0, group_size, backward_horner_step, jnp.zeros_like(first_state))


def powers_of(matrices, top):
    eye = jnp.broadcast_to(jnp.eye(matrices.shape[1], dtype=matrices.dtype), matrices.shape)
    found = [eye, matrices]
    while len(found) <= top:
        reached = found[-1]
        more = jnp.einsum("pij,bpjk->bpik", reached, jnp.stack(found[1:]), precision=HIGHEST)
        found.extend(list(more))
    return jnp.stack(found[: top + 1])


def forward_sum(spread):
    rows = spread.shape[0]
    total = spread[:, 0]
    for lag in range(1, rows):
        total = total + jnp.pad(spread[: rows - lag, lag], ((lag, 0), (0, 0)))
    return total


def backward_sum(spread):
    rows = spread.shape[0]
    total = spread[:, 0]
    for lag in range(1, rows):
        total = total + jnp.pad(spread[lag:, lag], ((0, lag), (0, 0)))
    return total


def by_powers(rows_in, power_stack):
    return jnp.einsum("kr,jsr->kjs", rows_in, power_stack, precision=HIGH)


def kalman(partial_value, filter_trans, filter_gain, transition, smooth_gain):
    rows, width = partial_value.shape
    block = lax.axis_index("tm")
    blocks = lax.axis_size("tm")
    last_device = block == blocks - 1
    both_powers = powers_of(jnp.stack((filter_trans, smooth_gain)), rows)
    filter_powers = both_powers[:, 0]
    smooth_powers = both_powers[:, 1]
    both_strides = powers_of(both_powers[rows], blocks - 1)
    filter_strides = both_strides[:, 0]
    smooth_strides = both_strides[:, 1]
    eye = jnp.eye(width, dtype=jnp.float32)
    correction = eye - product(smooth_gain, transition)
    carried = jnp.einsum(
        "tij,tjk->tik",
        smooth_powers[:rows],
        jnp.einsum("ij,tjk->tik", correction, filter_powers[1:], precision=HIGHEST),
        precision=HIGHEST,
    )
    lead_map = jnp.sum(carried, axis=0)
    tail_fix = product(smooth_powers[rows - 1], product(eye - correction, filter_powers[rows]))
    last_map = lead_map + tail_fix

    drive = product(partial_value, filter_gain.T)
    own_run = forward_sum(by_powers(drive, filter_powers[:rows]))
    own_back = backward_terms(own_run, transition, smooth_gain, last_device)
    own_smooth = backward_sum(by_powers(own_back, smooth_powers[:rows]))
    own_ends = jnp.concatenate((own_run[rows - 1], own_smooth[0]))[None]
    every_end = collect(own_ends, ("tm", "od"), 0)
    ends = jnp.sum(every_end.reshape(blocks, -1, 2 * width), axis=1)
    ends, own_run = lax.optimization_barrier((ends, own_run))
    filter_ends = ends[:, :width]
    smooth_starts = ends[:, width:]

    stride_ids = lax.broadcasted_iota(jnp.int32, (blocks, blocks, blocks), 1)
    source_ids = lax.broadcasted_iota(jnp.int32, (blocks, blocks, blocks), 2)
    target_ids = lax.broadcasted_iota(jnp.int32, (blocks, blocks, blocks), 0)
    pick = (stride_ids == target_ids - 1 - source_ids).astype(jnp.float32)
    spread_ends = jnp.einsum("msr,kr->mks", filter_strides, filter_ends, precision=HIGH)
    starts = jnp.einsum("bmk,mks->bs", pick, spread_ends, precision=HIGHEST)
    block_ids = lax.broadcasted_iota(jnp.int32, (blocks, width), 0)
    through = jnp.where(
        block_ids == blocks - 1, product(starts, last_map.T), product(starts, lead_map.T)
    )
    smooth_full = smooth_starts + through
    spread_starts = jnp.einsum("msr,kr->mks", smooth_strides, smooth_full, precision=HIGH)
    mk_stride = lax.broadcasted_iota(jnp.int32, (blocks, blocks), 0)
    mk_source = lax.broadcasted_iota(jnp.int32, (blocks, blocks), 1)
    later_pick = (mk_stride == mk_source - block - 1).astype(jnp.float32)
    end_state = jnp.einsum("mk,mks->s", later_pick, spread_starts, precision=HIGHEST)
    own_pick = (lax.broadcasted_iota(jnp.int32, (blocks,), 0) == block).astype(jnp.float32)
    start_state = jnp.einsum("b,bs->s", own_pick, starts, precision=HIGHEST)

    zero_run = over_copies(own_run, "od")
    filtered = zero_run + jnp.einsum("jsr,r->js", filter_powers[1:], start_state, precision=HIGH)
    back_terms = backward_terms(filtered, transition, smooth_gain, last_device)
    local_smooth = backward_sum(by_powers(back_terms, smooth_powers[:rows]))
    carried_end = jnp.einsum("jsr,r->js", smooth_powers[1:], end_state, precision=HIGH)
    smoothed = local_smooth + jnp.flip(carried_end, axis=0)
    return filtered, smoothed


GROUPS = (16, 4)


def mttkrp_kernel(coords_ref, counts_ref, tiles_ref, table_ref, out_ref, orig_ref):
    step = pl.program_id(0)
    slot_total = tiles_ref.shape[1]
    tile_side = tiles_ref.shape[2]
    state_width = orig_ref.shape[1]
    tile_top = table_ref.shape[0] // tile_side - 1

    @pl.when(step == 0)
    def _():
        orig_ref[...] = table_ref[:, pl.ds(0, state_width)].astype(jnp.float32)

    live = jnp.clip(counts_ref[step], 0, slot_total)

    def slot_term(slot):
        orig_id = jnp.clip(coords_ref[0, step, slot], 0, tile_top)
        dest_id = jnp.clip(coords_ref[1, step, slot], 0, tile_top)
        dest_start = pl.multiple_of(dest_id * tile_side, tile_side)
        orig_start = pl.multiple_of(orig_id * tile_side, tile_side)
        dest_rows = table_ref[pl.ds(dest_start, tile_side), pl.ds(state_width, state_width)]
        orig_rows = orig_ref[pl.ds(orig_start, tile_side), :]
        tile_dest = jnp.dot(tiles_ref[0, slot], dest_rows, preferred_element_type=jnp.float32)
        weighted = tile_dest * orig_rows
        return jnp.sum(weighted.reshape(tile_side // 8, 8, state_width), axis=0)

    def group_of(width, first):
        def one_group(group, acc):
            terms = [slot_term(first + group * width + k) for k in range(width)]
            while len(terms) > 1:
                terms = [terms[k] + terms[k + 1] for k in range(0, len(terms), 2)]
            return acc + terms[0]

        return one_group

    def one_slot(slot, acc):
        return acc + slot_term(slot)

    acc = jnp.zeros((8, state_width), jnp.float32)
    done = 0
    for width in GROUPS:
        groups = (live - done) // width
        acc = lax.fori_loop(0, groups, group_of(width, done), acc)
        done = done + groups * width
    acc = lax.fori_loop(done, live, one_slot, acc)
    out_ref[0] = jnp.sum(acc, axis=0, keepdims=True)


def mttkrp(tiles, coords, live_counts, table):
    step_count, slot_count, tile_side, _ = tiles.shape
    state_width = table.shape[1] // 2
    grid_spec = pltpu.PrefetchScalarGridSpec(
        num_scalar_prefetch=2,
        grid=(step_count,),
        in_specs=[
            pl.BlockSpec((1, slot_count, tile_side, tile_side), lambda t, c, n: (t, 0, 0, 0)),
            pl.BlockSpec(table.shape, lambda t, c, n: (0, 0)),
        ],
        out_specs=pl.BlockSpec((1, 1, state_width), lambda t, c, n: (t, 0, 0)),
        scratch_shapes=[pltpu.VMEM((table.shape[0], state_width), jnp.float32)],
    )
    out = pl.pallas_call(
        mttkrp_kernel,
        grid_spec=grid_spec,
        out_shape=jax.ShapeDtypeStruct((step_count, 1, state_width), jnp.float32),
        compiler_params=pltpu.CompilerParams(dimension_semantics=("arbitrary",)),
    )(coords, live_counts, tiles, table)
    return out.reshape(step_count, state_width)


def local(
    tiles,
    coords,
    counts,
    anchor_factor,
    dest_factor,
    filter_trans,
    filter_gain,
    transition,
    smooth_gain,
):
    state_width = anchor_factor.shape[1]
    table = collect(jnp.concatenate((anchor_factor, dest_factor), axis=1), ("tm", "od"), 0)
    partial_value = mttkrp(tiles, coords, counts[:, 0], table)
    return kalman(partial_value, filter_trans, filter_gain, transition, smooth_gain)


def solution(mesh):
    return jax.shard_map(
        local,
        mesh=mesh,
        in_specs=(
            P("tm", "od", None, None),
            P(None, "tm", "od"),
            P("tm", "od"),
            P(("tm", "od"), None),
            P(("tm", "od"), None),
            P(),
            P(),
            P(),
            P(),
        ),
        out_specs=(P("tm", None), P("tm", None)),
        check_vma=False,
    )
```

```python
import jax
import jax.numpy as jnp
from jax import lax
from jax.sharding import PartitionSpec as P
from jax.experimental import pallas as pl
from jax.experimental.pallas import tpu as pltpu

HIGHEST = lax.Precision.HIGHEST
HIGH = lax.Precision.HIGH


def joined_along(pieces, dim):
    shape = list(pieces.shape[1:])
    shape[dim] *= pieces.shape[0]
    return jnp.moveaxis(pieces, 0, dim).reshape(shape)


def from_everyone(array, axis):
    size = lax.axis_size(axis)
    return lax.all_to_all(
        jnp.broadcast_to(array[None], (size, *array.shape)), axis, 0, 0, tiled=True
    )


def collect(array, axis, dim):
    return joined_along(from_everyone(array, axis), dim)


def in_one_piece(arrays, axis, dim, along):
    widths = [a.shape[along] for a in arrays]
    both = jnp.concatenate(arrays, axis=along)
    filled = lax.all_gather(both, axis, axis=dim, tiled=True)
    return tuple(jnp.split(filled, [sum(widths[:k]) for k in range(1, len(widths))], axis=along))


def over_copies(array, axis):
    everything = from_everyone(array, axis)
    return jnp.sum(everything, axis=0)


def product(left_mat, right_mat):
    return jnp.dot(left_mat, right_mat, precision=HIGHEST)


def matrix_power(matrix, exponent):
    result = None
    squared = matrix
    while exponent > 0:
        if exponent % 2 == 1:
            result = squared
        exponent = exponent // 2
        if exponent > 0:
            squared = product(squared, squared)
    return result


def run_rows(start_state, drive, matrix, reverse):

    def advance(carried, drive_row):
        updated = jnp.dot(matrix, carried, precision=HIGHEST) + drive_row
        return (updated, updated)

    return lax.scan(advance, start_state, drive, reverse=reverse)[1]


def backward_terms(filtered, transition, smooth_gain, last_device):
    predicted = product(filtered, transition.T)
    back_terms = filtered - product(predicted, smooth_gain.T)
    row_ids = lax.broadcasted_iota(jnp.int32, back_terms.shape, 0)
    final_row = jnp.logical_and(last_device, row_ids == back_terms.shape[0] - 1)
    return jnp.where(final_row, filtered, back_terms)


def forward_start(stride, last_state):
    states = collect(last_state[None], "tm", 0)
    own_index = lax.axis_index("tm")

    def forward_horner_step(position, running):
        stepped = jnp.dot(stride, running, precision=HIGHEST) + states[position]
        return jnp.where(position < own_index, stepped, running)

    return lax.fori_loop(0, lax.axis_size("tm"), forward_horner_step, jnp.zeros_like(last_state))


def backward_start(stride, first_state):
    states = collect(first_state[None], "tm", 0)
    own_index = lax.axis_index("tm")
    group_size = lax.axis_size("tm")

    def backward_horner_step(turn, running):
        position = group_size - 1 - turn
        stepped = jnp.dot(stride, running, precision=HIGHEST) + states[position]
        return jnp.where(position > own_index, stepped, running)

    return lax.fori_loop(0, group_size, backward_horner_step, jnp.zeros_like(first_state))


def powers_of(matrices, top):
    eye = jnp.broadcast_to(jnp.eye(matrices.shape[1], dtype=matrices.dtype), matrices.shape)
    found = [eye, matrices]
    while len(found) <= top:
        reached = found[-1]
        more = jnp.einsum("pij,bpjk->bpik", reached, jnp.stack(found[1:]), precision=HIGHEST)
        found.extend(list(more))
    return jnp.stack(found[: top + 1])


def forward_sum(spread):
    rows = spread.shape[0]
    total = spread[:, 0]
    for lag in range(1, rows):
        total = total + jnp.pad(spread[: rows - lag, lag], ((lag, 0), (0, 0)))
    return total


def backward_sum(spread):
    rows = spread.shape[0]
    total = spread[:, 0]
    for lag in range(1, rows):
        total = total + jnp.pad(spread[lag:, lag], ((0, lag), (0, 0)))
    return total


def by_powers(rows_in, power_stack):
    return jnp.einsum("kr,jsr->kjs", rows_in, power_stack, precision=HIGH)


def kalman(partial_value, filter_trans, filter_gain, transition, smooth_gain):
    rows, width = partial_value.shape
    block = lax.axis_index("tm")
    blocks = lax.axis_size("tm")
    last_device = block == blocks - 1
    both_powers = powers_of(jnp.stack((filter_trans, smooth_gain)), rows)
    filter_powers = both_powers[:, 0]
    smooth_powers = both_powers[:, 1]
    both_strides = powers_of(both_powers[rows], blocks - 1)
    filter_strides = both_strides[:, 0]
    smooth_strides = both_strides[:, 1]
    eye = jnp.eye(width, dtype=jnp.float32)
    correction = eye - product(smooth_gain, transition)
    carried = jnp.einsum(
        "tij,tjk->tik",
        smooth_powers[:rows],
        jnp.einsum("ij,tjk->tik", correction, filter_powers[1:], precision=HIGHEST),
        precision=HIGHEST,
    )
    lead_map = jnp.sum(carried, axis=0)
    tail_fix = product(smooth_powers[rows - 1], product(eye - correction, filter_powers[rows]))
    last_map = lead_map + tail_fix

    observed = over_copies(partial_value, "od")
    drive = product(observed, filter_gain.T)
    zero_run = forward_sum(by_powers(drive, filter_powers[:rows]))
    zero_back = backward_terms(zero_run, transition, smooth_gain, last_device)
    zero_smooth = backward_sum(by_powers(zero_back, smooth_powers[:rows]))
    ends = lax.all_gather(
        jnp.concatenate((zero_run[rows - 1], zero_smooth[0]))[None], "tm", axis=0, tiled=True
    )
    filter_ends = ends[:, :width]
    smooth_starts = ends[:, width:]

    stride_ids = lax.broadcasted_iota(jnp.int32, (blocks, blocks, blocks), 1)
    source_ids = lax.broadcasted_iota(jnp.int32, (blocks, blocks, blocks), 2)
    target_ids = lax.broadcasted_iota(jnp.int32, (blocks, blocks, blocks), 0)
    pick = (stride_ids == target_ids - 1 - source_ids).astype(jnp.float32)
    spread_ends = jnp.einsum("msr,kr->mks", filter_strides, filter_ends, precision=HIGH)
    starts = jnp.einsum("bmk,mks->bs", pick, spread_ends, precision=HIGHEST)
    block_ids = lax.broadcasted_iota(jnp.int32, (blocks, width), 0)
    through = jnp.where(
        block_ids == blocks - 1, product(starts, last_map.T), product(starts, lead_map.T)
    )
    smooth_full = smooth_starts + through
    spread_starts = jnp.einsum("msr,kr->mks", smooth_strides, smooth_full, precision=HIGH)
    mk_stride = lax.broadcasted_iota(jnp.int32, (blocks, blocks), 0)
    mk_source = lax.broadcasted_iota(jnp.int32, (blocks, blocks), 1)
    later_pick = (mk_stride == mk_source - block - 1).astype(jnp.float32)
    end_state = jnp.einsum("mk,mks->s", later_pick, spread_starts, precision=HIGHEST)
    own_pick = (lax.broadcasted_iota(jnp.int32, (blocks,), 0) == block).astype(jnp.float32)
    start_state = jnp.einsum("b,bs->s", own_pick, starts, precision=HIGHEST)

    filtered = zero_run + jnp.einsum("jsr,r->js", filter_powers[1:], start_state, precision=HIGH)
    back_terms = backward_terms(filtered, transition, smooth_gain, last_device)
    local_smooth = backward_sum(by_powers(back_terms, smooth_powers[:rows]))
    carried_end = jnp.einsum("jsr,r->js", smooth_powers[1:], end_state, precision=HIGH)
    smoothed = local_smooth + jnp.flip(carried_end, axis=0)
    return filtered, smoothed


GROUPS = (32, 8, 4)


def mttkrp_kernel(coords_ref, counts_ref, tiles_ref, table_ref, out_ref, orig_ref):
    step = pl.program_id(0)
    slot_total = tiles_ref.shape[1]
    tile_side = tiles_ref.shape[2]
    state_width = orig_ref.shape[1]
    tile_top = table_ref.shape[0] // tile_side - 1

    @pl.when(step == 0)
    def _():
        orig_ref[...] = table_ref[:, pl.ds(0, state_width)].astype(jnp.float32)

    live = jnp.clip(counts_ref[step], 0, slot_total)

    def slot_term(slot):
        orig_id = jnp.clip(coords_ref[0, step, slot], 0, tile_top)
        dest_id = jnp.clip(coords_ref[1, step, slot], 0, tile_top)
        dest_start = pl.multiple_of(dest_id * tile_side, tile_side)
        orig_start = pl.multiple_of(orig_id * tile_side, tile_side)
        dest_rows = table_ref[pl.ds(dest_start, tile_side), pl.ds(state_width, state_width)]
        orig_rows = orig_ref[pl.ds(orig_start, tile_side), :]
        tile_dest = jnp.dot(tiles_ref[0, slot], dest_rows, preferred_element_type=jnp.float32)
        weighted = tile_dest * orig_rows
        return jnp.sum(weighted.reshape(tile_side // 8, 8, state_width), axis=0)

    def group_of(width, first):
        def one_group(group, acc):
            terms = [slot_term(first + group * width + k) for k in range(width)]
            while len(terms) > 1:
                terms = [terms[k] + terms[k + 1] for k in range(0, len(terms), 2)]
            return acc + terms[0]

        return one_group

    def one_slot(slot, acc):
        return acc + slot_term(slot)

    acc = jnp.zeros((8, state_width), jnp.float32)
    done = 0
    for width in GROUPS:
        groups = (live - done) // width
        acc = lax.fori_loop(0, groups, group_of(width, done), acc)
        done = done + groups * width
    acc = lax.fori_loop(done, live, one_slot, acc)
    out_ref[0] = jnp.sum(acc, axis=0, keepdims=True)


def mttkrp(tiles, coords, live_counts, table):
    step_count, slot_count, tile_side, _ = tiles.shape
    state_width = table.shape[1] // 2
    grid_spec = pltpu.PrefetchScalarGridSpec(
        num_scalar_prefetch=2,
        grid=(step_count,),
        in_specs=[
            pl.BlockSpec((1, slot_count, tile_side, tile_side), lambda t, c, n: (t, 0, 0, 0)),
            pl.BlockSpec(table.shape, lambda t, c, n: (0, 0)),
        ],
        out_specs=pl.BlockSpec((1, 1, state_width), lambda t, c, n: (t, 0, 0)),
        scratch_shapes=[pltpu.VMEM((table.shape[0], state_width), jnp.float32)],
    )
    out = pl.pallas_call(
        mttkrp_kernel,
        grid_spec=grid_spec,
        out_shape=jax.ShapeDtypeStruct((step_count, 1, state_width), jnp.float32),
        compiler_params=pltpu.CompilerParams(dimension_semantics=("arbitrary",)),
    )(coords, live_counts, tiles, table)
    return out.reshape(step_count, state_width)


def local(
    tiles,
    coords,
    counts,
    anchor_factor,
    dest_factor,
    filter_trans,
    filter_gain,
    transition,
    smooth_gain,
):
    state_width = anchor_factor.shape[1]
    table = collect(jnp.concatenate((anchor_factor, dest_factor), axis=1), ("tm", "od"), 0)
    partial_value = mttkrp(tiles, coords, counts[:, 0], table)
    return kalman(partial_value, filter_trans, filter_gain, transition, smooth_gain)


def solution(mesh):
    return jax.shard_map(
        local,
        mesh=mesh,
        in_specs=(
            P("tm", "od", None, None),
            P(None, "tm", "od"),
            P("tm", "od"),
            P(("tm", "od"), None),
            P(("tm", "od"), None),
            P(),
            P(),
            P(),
            P(),
        ),
        out_specs=(P("tm", None), P("tm", None)),
        check_vma=False,
    )
```

```python
import jax
import jax.numpy as jnp
from jax import lax
from jax.sharding import PartitionSpec as P
from jax.experimental import pallas as pl
from jax.experimental.pallas import tpu as pltpu

HIGHEST = lax.Precision.HIGHEST
HIGH = lax.Precision.HIGH


def joined_along(pieces, dim):
    shape = list(pieces.shape[1:])
    shape[dim] *= pieces.shape[0]
    return jnp.moveaxis(pieces, 0, dim).reshape(shape)


def from_everyone(array, axis):
    size = lax.axis_size(axis)
    return lax.all_to_all(
        jnp.broadcast_to(array[None], (size, *array.shape)), axis, 0, 0, tiled=True
    )


def collect(array, axis, dim):
    return joined_along(from_everyone(array, axis), dim)


def in_one_piece(arrays, axis, dim, along):
    widths = [a.shape[along] for a in arrays]
    both = jnp.concatenate(arrays, axis=along)
    filled = lax.all_gather(both, axis, axis=dim, tiled=True)
    return tuple(jnp.split(filled, [sum(widths[:k]) for k in range(1, len(widths))], axis=along))


def over_copies(array, axis):
    everything = from_everyone(array, axis)
    return jnp.sum(everything, axis=0)


def product(left_mat, right_mat):
    return jnp.dot(left_mat, right_mat, precision=HIGHEST)


def matrix_power(matrix, exponent):
    result = None
    squared = matrix
    while exponent > 0:
        if exponent % 2 == 1:
            result = squared
        exponent = exponent // 2
        if exponent > 0:
            squared = product(squared, squared)
    return result


def run_rows(start_state, drive, matrix, reverse):

    def advance(carried, drive_row):
        updated = jnp.dot(matrix, carried, precision=HIGHEST) + drive_row
        return (updated, updated)

    return lax.scan(advance, start_state, drive, reverse=reverse)[1]


def backward_terms(filtered, transition, smooth_gain, last_device):
    predicted = product(filtered, transition.T)
    back_terms = filtered - product(predicted, smooth_gain.T)
    row_ids = lax.broadcasted_iota(jnp.int32, back_terms.shape, 0)
    final_row = jnp.logical_and(last_device, row_ids == back_terms.shape[0] - 1)
    return jnp.where(final_row, filtered, back_terms)


def forward_start(stride, last_state):
    states = collect(last_state[None], "tm", 0)
    own_index = lax.axis_index("tm")

    def forward_horner_step(position, running):
        stepped = jnp.dot(stride, running, precision=HIGHEST) + states[position]
        return jnp.where(position < own_index, stepped, running)

    return lax.fori_loop(0, lax.axis_size("tm"), forward_horner_step, jnp.zeros_like(last_state))


def backward_start(stride, first_state):
    states = collect(first_state[None], "tm", 0)
    own_index = lax.axis_index("tm")
    group_size = lax.axis_size("tm")

    def backward_horner_step(turn, running):
        position = group_size - 1 - turn
        stepped = jnp.dot(stride, running, precision=HIGHEST) + states[position]
        return jnp.where(position > own_index, stepped, running)

    return lax.fori_loop(0, group_size, backward_horner_step, jnp.zeros_like(first_state))


def powers_of(matrices, top):
    eye = jnp.broadcast_to(jnp.eye(matrices.shape[1], dtype=matrices.dtype), matrices.shape)
    found = [eye, matrices]
    while len(found) <= top:
        reached = found[-1]
        more = jnp.einsum("pij,bpjk->bpik", reached, jnp.stack(found[1:]), precision=HIGHEST)
        found.extend(list(more))
    return jnp.stack(found[: top + 1])


def forward_sum(spread):
    rows = spread.shape[0]
    total = spread[:, 0]
    for lag in range(1, rows):
        total = total + jnp.pad(spread[: rows - lag, lag], ((lag, 0), (0, 0)))
    return total


def backward_sum(spread):
    rows = spread.shape[0]
    total = spread[:, 0]
    for lag in range(1, rows):
        total = total + jnp.pad(spread[lag:, lag], ((0, lag), (0, 0)))
    return total


def by_powers(rows_in, power_stack):
    return jnp.einsum("kr,jsr->kjs", rows_in, power_stack, precision=HIGH)


def kalman(partial_value, filter_trans, filter_gain, transition, smooth_gain):
    rows, width = partial_value.shape
    block = lax.axis_index("tm")
    blocks = lax.axis_size("tm")
    last_device = block == blocks - 1
    both_powers = powers_of(jnp.stack((filter_trans, smooth_gain)), rows)
    filter_powers = both_powers[:, 0]
    smooth_powers = both_powers[:, 1]
    both_strides = powers_of(both_powers[rows], blocks - 1)
    filter_strides = both_strides[:, 0]
    smooth_strides = both_strides[:, 1]
    eye = jnp.eye(width, dtype=jnp.float32)
    correction = eye - product(smooth_gain, transition)
    carried = jnp.einsum(
        "tij,tjk->tik",
        smooth_powers[:rows],
        jnp.einsum("ij,tjk->tik", correction, filter_powers[1:], precision=HIGHEST),
        precision=HIGHEST,
    )
    lead_map = jnp.sum(carried, axis=0)
    tail_fix = product(smooth_powers[rows - 1], product(eye - correction, filter_powers[rows]))
    last_map = lead_map + tail_fix

    observed = over_copies(partial_value, "od")
    drive = product(observed, filter_gain.T)
    zero_run = forward_sum(by_powers(drive, filter_powers[:rows]))
    zero_back = backward_terms(zero_run, transition, smooth_gain, last_device)
    zero_smooth = backward_sum(by_powers(zero_back, smooth_powers[:rows]))
    ends = collect(jnp.concatenate((zero_run[rows - 1], zero_smooth[0]))[None], "tm", 0)
    filter_ends = ends[:, :width]
    smooth_starts = ends[:, width:]

    stride_ids = lax.broadcasted_iota(jnp.int32, (blocks, blocks, blocks), 1)
    source_ids = lax.broadcasted_iota(jnp.int32, (blocks, blocks, blocks), 2)
    target_ids = lax.broadcasted_iota(jnp.int32, (blocks, blocks, blocks), 0)
    pick = (stride_ids == target_ids - 1 - source_ids).astype(jnp.float32)
    spread_ends = jnp.einsum("msr,kr->mks", filter_strides, filter_ends, precision=HIGH)
    starts = jnp.einsum("bmk,mks->bs", pick, spread_ends, precision=HIGHEST)
    block_ids = lax.broadcasted_iota(jnp.int32, (blocks, width), 0)
    through = jnp.where(
        block_ids == blocks - 1, product(starts, last_map.T), product(starts, lead_map.T)
    )
    smooth_full = smooth_starts + through
    spread_starts = jnp.einsum("msr,kr->mks", smooth_strides, smooth_full, precision=HIGH)
    mk_stride = lax.broadcasted_iota(jnp.int32, (blocks, blocks), 0)
    mk_source = lax.broadcasted_iota(jnp.int32, (blocks, blocks), 1)
    later_pick = (mk_stride == mk_source - block - 1).astype(jnp.float32)
    end_state = jnp.einsum("mk,mks->s", later_pick, spread_starts, precision=HIGHEST)
    own_pick = (lax.broadcasted_iota(jnp.int32, (blocks,), 0) == block).astype(jnp.float32)
    start_state = jnp.einsum("b,bs->s", own_pick, starts, precision=HIGHEST)

    filtered = zero_run + jnp.einsum("jsr,r->js", filter_powers[1:], start_state, precision=HIGH)
    back_terms = backward_terms(filtered, transition, smooth_gain, last_device)
    local_smooth = backward_sum(by_powers(back_terms, smooth_powers[:rows]))
    carried_end = jnp.einsum("jsr,r->js", smooth_powers[1:], end_state, precision=HIGH)
    smoothed = local_smooth + jnp.flip(carried_end, axis=0)
    return filtered, smoothed


GROUPS = (32, 8, 4)


def mttkrp_kernel(coords_ref, counts_ref, tiles_ref, table_ref, out_ref, orig_ref):
    step = pl.program_id(0)
    slot_total = tiles_ref.shape[1]
    tile_side = tiles_ref.shape[2]
    state_width = orig_ref.shape[1]
    tile_top = table_ref.shape[0] // tile_side - 1

    @pl.when(step == 0)
    def _():
        orig_ref[...] = table_ref[:, pl.ds(0, state_width)].astype(jnp.float32)

    live = jnp.clip(counts_ref[step], 0, slot_total)

    def slot_term(slot):
        orig_id = jnp.clip(coords_ref[0, step, slot], 0, tile_top)
        dest_id = jnp.clip(coords_ref[1, step, slot], 0, tile_top)
        dest_start = pl.multiple_of(dest_id * tile_side, tile_side)
        orig_start = pl.multiple_of(orig_id * tile_side, tile_side)
        dest_rows = table_ref[pl.ds(dest_start, tile_side), pl.ds(state_width, state_width)]
        orig_rows = orig_ref[pl.ds(orig_start, tile_side), :]
        tile_dest = jnp.dot(tiles_ref[0, slot], dest_rows, preferred_element_type=jnp.float32)
        weighted = tile_dest * orig_rows
        return jnp.sum(weighted.reshape(tile_side // 8, 8, state_width), axis=0)

    def group_of(width, first):
        def one_group(group, acc):
            terms = [slot_term(first + group * width + k) for k in range(width)]
            while len(terms) > 1:
                terms = [terms[k] + terms[k + 1] for k in range(0, len(terms), 2)]
            return acc + terms[0]

        return one_group

    def one_slot(slot, acc):
        return acc + slot_term(slot)

    acc = jnp.zeros((8, state_width), jnp.float32)
    done = 0
    for width in GROUPS:
        groups = (live - done) // width
        acc = lax.fori_loop(0, groups, group_of(width, done), acc)
        done = done + groups * width
    acc = lax.fori_loop(done, live, one_slot, acc)
    out_ref[0] = jnp.sum(acc, axis=0, keepdims=True)


def mttkrp(tiles, coords, live_counts, table):
    step_count, slot_count, tile_side, _ = tiles.shape
    state_width = table.shape[1] // 2
    grid_spec = pltpu.PrefetchScalarGridSpec(
        num_scalar_prefetch=2,
        grid=(step_count,),
        in_specs=[
            pl.BlockSpec((1, slot_count, tile_side, tile_side), lambda t, c, n: (t, 0, 0, 0)),
            pl.BlockSpec(table.shape, lambda t, c, n: (0, 0)),
        ],
        out_specs=pl.BlockSpec((1, 1, state_width), lambda t, c, n: (t, 0, 0)),
        scratch_shapes=[pltpu.VMEM((table.shape[0], state_width), jnp.float32)],
    )
    out = pl.pallas_call(
        mttkrp_kernel,
        grid_spec=grid_spec,
        out_shape=jax.ShapeDtypeStruct((step_count, 1, state_width), jnp.float32),
        compiler_params=pltpu.CompilerParams(dimension_semantics=("arbitrary",)),
    )(coords, live_counts, tiles, table)
    return out.reshape(step_count, state_width)


def local(
    tiles,
    coords,
    counts,
    anchor_factor,
    dest_factor,
    filter_trans,
    filter_gain,
    transition,
    smooth_gain,
):
    state_width = anchor_factor.shape[1]
    table = collect(jnp.concatenate((anchor_factor, dest_factor), axis=1), ("tm", "od"), 0)
    partial_value = mttkrp(tiles, coords, counts[:, 0], table)
    return kalman(partial_value, filter_trans, filter_gain, transition, smooth_gain)


def solution(mesh):
    return jax.shard_map(
        local,
        mesh=mesh,
        in_specs=(
            P("tm", "od", None, None),
            P(None, "tm", "od"),
            P("tm", "od"),
            P(("tm", "od"), None),
            P(("tm", "od"), None),
            P(),
            P(),
            P(),
            P(),
        ),
        out_specs=(P("tm", None), P("tm", None)),
        check_vma=False,
    )
```

```python
import jax
import jax.numpy as jnp
from jax import lax
from jax.sharding import PartitionSpec as P
from jax.experimental import pallas as pl
from jax.experimental.pallas import tpu as pltpu

HIGHEST = lax.Precision.HIGHEST
HIGH = lax.Precision.HIGH


def joined_along(pieces, dim):
    shape = list(pieces.shape[1:])
    shape[dim] *= pieces.shape[0]
    return jnp.moveaxis(pieces, 0, dim).reshape(shape)


def from_everyone(array, axis):
    size = lax.axis_size(axis)
    return lax.all_to_all(
        jnp.broadcast_to(array[None], (size, *array.shape)), axis, 0, 0, tiled=True
    )


def collect(array, axis, dim):
    return joined_along(from_everyone(array, axis), dim)


def in_one_piece(arrays, axis, dim, along):
    widths = [a.shape[along] for a in arrays]
    both = jnp.concatenate(arrays, axis=along)
    filled = lax.all_gather(both, axis, axis=dim, tiled=True)
    return tuple(jnp.split(filled, [sum(widths[:k]) for k in range(1, len(widths))], axis=along))


def over_copies(array, axis):
    everything = from_everyone(array, axis)
    return jnp.sum(everything, axis=0)


def product(left_mat, right_mat):
    return jnp.dot(left_mat, right_mat, precision=HIGHEST)


def matrix_power(matrix, exponent):
    result = None
    squared = matrix
    while exponent > 0:
        if exponent % 2 == 1:
            result = squared
        exponent = exponent // 2
        if exponent > 0:
            squared = product(squared, squared)
    return result


def run_rows(start_state, drive, matrix, reverse):

    def advance(carried, drive_row):
        updated = jnp.dot(matrix, carried, precision=HIGHEST) + drive_row
        return (updated, updated)

    return lax.scan(advance, start_state, drive, reverse=reverse)[1]


def backward_terms(filtered, transition, smooth_gain, last_device):
    predicted = product(filtered, transition.T)
    back_terms = filtered - product(predicted, smooth_gain.T)
    row_ids = lax.broadcasted_iota(jnp.int32, back_terms.shape, 0)
    final_row = jnp.logical_and(last_device, row_ids == back_terms.shape[0] - 1)
    return jnp.where(final_row, filtered, back_terms)


def forward_start(stride, last_state):
    states = collect(last_state[None], "tm", 0)
    own_index = lax.axis_index("tm")

    def forward_horner_step(position, running):
        stepped = jnp.dot(stride, running, precision=HIGHEST) + states[position]
        return jnp.where(position < own_index, stepped, running)

    return lax.fori_loop(0, lax.axis_size("tm"), forward_horner_step, jnp.zeros_like(last_state))


def backward_start(stride, first_state):
    states = collect(first_state[None], "tm", 0)
    own_index = lax.axis_index("tm")
    group_size = lax.axis_size("tm")

    def backward_horner_step(turn, running):
        position = group_size - 1 - turn
        stepped = jnp.dot(stride, running, precision=HIGHEST) + states[position]
        return jnp.where(position > own_index, stepped, running)

    return lax.fori_loop(0, group_size, backward_horner_step, jnp.zeros_like(first_state))


def powers_of(matrices, top):
    eye = jnp.broadcast_to(jnp.eye(matrices.shape[1], dtype=matrices.dtype), matrices.shape)
    found = [eye, matrices]
    while len(found) <= top:
        reached = found[-1]
        more = jnp.einsum("pij,bpjk->bpik", reached, jnp.stack(found[1:]), precision=HIGHEST)
        found.extend(list(more))
    return jnp.stack(found[: top + 1])


def forward_sum(spread):
    rows = spread.shape[0]
    total = spread[:, 0]
    for lag in range(1, rows):
        total = total + jnp.pad(spread[: rows - lag, lag], ((lag, 0), (0, 0)))
    return total


def backward_sum(spread):
    rows = spread.shape[0]
    total = spread[:, 0]
    for lag in range(1, rows):
        total = total + jnp.pad(spread[lag:, lag], ((0, lag), (0, 0)))
    return total


def by_powers(rows_in, power_stack):
    return jnp.einsum("kr,jsr->kjs", rows_in, power_stack, precision=HIGH)


def kalman(partial_value, filter_trans, filter_gain, transition, smooth_gain):
    rows, width = partial_value.shape
    block = lax.axis_index("tm")
    blocks = lax.axis_size("tm")
    last_device = block == blocks - 1
    both_powers = powers_of(jnp.stack((filter_trans, smooth_gain)), rows)
    filter_powers = both_powers[:, 0]
    smooth_powers = both_powers[:, 1]
    both_strides = powers_of(both_powers[rows], blocks - 1)
    filter_strides = both_strides[:, 0]
    smooth_strides = both_strides[:, 1]
    eye = jnp.eye(width, dtype=jnp.float32)
    correction = eye - product(smooth_gain, transition)
    carried = jnp.einsum(
        "tij,tjk->tik",
        smooth_powers[:rows],
        jnp.einsum("ij,tjk->tik", correction, filter_powers[1:], precision=HIGH),
        precision=HIGH,
    )
    lead_map = jnp.sum(carried, axis=0)
    tail_fix = product(smooth_powers[rows - 1], product(eye - correction, filter_powers[rows]))
    last_map = lead_map + tail_fix

    observed = over_copies(partial_value, "od")
    drive = product(observed, filter_gain.T)
    zero_run = forward_sum(by_powers(drive, filter_powers[:rows]))
    zero_back = backward_terms(zero_run, transition, smooth_gain, last_device)
    zero_smooth = backward_sum(by_powers(zero_back, smooth_powers[:rows]))
    ends = collect(jnp.concatenate((zero_run[rows - 1], zero_smooth[0]))[None], "tm", 0)
    filter_ends = ends[:, :width]
    smooth_starts = ends[:, width:]

    stride_ids = lax.broadcasted_iota(jnp.int32, (blocks, blocks, blocks), 1)
    source_ids = lax.broadcasted_iota(jnp.int32, (blocks, blocks, blocks), 2)
    target_ids = lax.broadcasted_iota(jnp.int32, (blocks, blocks, blocks), 0)
    pick = (stride_ids == target_ids - 1 - source_ids).astype(jnp.float32)
    spread_ends = jnp.einsum("msr,kr->mks", filter_strides, filter_ends, precision=HIGH)
    starts = jnp.einsum("bmk,mks->bs", pick, spread_ends, precision=HIGHEST)
    block_ids = lax.broadcasted_iota(jnp.int32, (blocks, width), 0)
    through = jnp.where(
        block_ids == blocks - 1, product(starts, last_map.T), product(starts, lead_map.T)
    )
    smooth_full = smooth_starts + through
    spread_starts = jnp.einsum("msr,kr->mks", smooth_strides, smooth_full, precision=HIGH)
    mk_stride = lax.broadcasted_iota(jnp.int32, (blocks, blocks), 0)
    mk_source = lax.broadcasted_iota(jnp.int32, (blocks, blocks), 1)
    later_pick = (mk_stride == mk_source - block - 1).astype(jnp.float32)
    end_state = jnp.einsum("mk,mks->s", later_pick, spread_starts, precision=HIGHEST)
    own_pick = (lax.broadcasted_iota(jnp.int32, (blocks,), 0) == block).astype(jnp.float32)
    start_state = jnp.einsum("b,bs->s", own_pick, starts, precision=HIGHEST)

    filtered = zero_run + jnp.einsum("jsr,r->js", filter_powers[1:], start_state, precision=HIGH)
    back_terms = backward_terms(filtered, transition, smooth_gain, last_device)
    local_smooth = backward_sum(by_powers(back_terms, smooth_powers[:rows]))
    carried_end = jnp.einsum("jsr,r->js", smooth_powers[1:], end_state, precision=HIGH)
    smoothed = local_smooth + jnp.flip(carried_end, axis=0)
    return filtered, smoothed


GROUPS = (32, 8, 4)


def mttkrp_kernel(coords_ref, counts_ref, tiles_ref, table_ref, out_ref, orig_ref):
    step = pl.program_id(0)
    slot_total = tiles_ref.shape[1]
    tile_side = tiles_ref.shape[2]
    state_width = orig_ref.shape[1]
    tile_top = table_ref.shape[0] // tile_side - 1

    @pl.when(step == 0)
    def _():
        orig_ref[...] = table_ref[:, pl.ds(0, state_width)].astype(jnp.float32)

    live = jnp.clip(counts_ref[step], 0, slot_total)

    def slot_term(slot):
        orig_id = jnp.clip(coords_ref[0, step, slot], 0, tile_top)
        dest_id = jnp.clip(coords_ref[1, step, slot], 0, tile_top)
        dest_start = pl.multiple_of(dest_id * tile_side, tile_side)
        orig_start = pl.multiple_of(orig_id * tile_side, tile_side)
        dest_rows = table_ref[pl.ds(dest_start, tile_side), pl.ds(state_width, state_width)]
        orig_rows = orig_ref[pl.ds(orig_start, tile_side), :]
        tile_dest = jnp.dot(tiles_ref[0, slot], dest_rows, preferred_element_type=jnp.float32)
        weighted = tile_dest * orig_rows
        return jnp.sum(weighted.reshape(tile_side // 8, 8, state_width), axis=0)

    def group_of(width, first):
        def one_group(group, acc):
            terms = [slot_term(first + group * width + k) for k in range(width)]
            while len(terms) > 1:
                terms = [terms[k] + terms[k + 1] for k in range(0, len(terms), 2)]
            return acc + terms[0]

        return one_group

    def one_slot(slot, acc):
        return acc + slot_term(slot)

    acc = jnp.zeros((8, state_width), jnp.float32)
    done = 0
    for width in GROUPS:
        groups = (live - done) // width
        acc = lax.fori_loop(0, groups, group_of(width, done), acc)
        done = done + groups * width
    acc = lax.fori_loop(done, live, one_slot, acc)
    out_ref[0] = jnp.sum(acc, axis=0, keepdims=True)


def mttkrp(tiles, coords, live_counts, table):
    step_count, slot_count, tile_side, _ = tiles.shape
    state_width = table.shape[1] // 2
    grid_spec = pltpu.PrefetchScalarGridSpec(
        num_scalar_prefetch=2,
        grid=(step_count,),
        in_specs=[
            pl.BlockSpec((1, slot_count, tile_side, tile_side), lambda t, c, n: (t, 0, 0, 0)),
            pl.BlockSpec(table.shape, lambda t, c, n: (0, 0)),
        ],
        out_specs=pl.BlockSpec((1, 1, state_width), lambda t, c, n: (t, 0, 0)),
        scratch_shapes=[pltpu.VMEM((table.shape[0], state_width), jnp.float32)],
    )
    out = pl.pallas_call(
        mttkrp_kernel,
        grid_spec=grid_spec,
        out_shape=jax.ShapeDtypeStruct((step_count, 1, state_width), jnp.float32),
        compiler_params=pltpu.CompilerParams(dimension_semantics=("arbitrary",)),
    )(coords, live_counts, tiles, table)
    return out.reshape(step_count, state_width)


def local(
    tiles,
    coords,
    counts,
    anchor_factor,
    dest_factor,
    filter_trans,
    filter_gain,
    transition,
    smooth_gain,
):
    state_width = anchor_factor.shape[1]
    table = collect(jnp.concatenate((anchor_factor, dest_factor), axis=1), ("tm", "od"), 0)
    partial_value = mttkrp(tiles, coords, counts[:, 0], table)
    return kalman(partial_value, filter_trans, filter_gain, transition, smooth_gain)


def solution(mesh):
    return jax.shard_map(
        local,
        mesh=mesh,
        in_specs=(
            P("tm", "od", None, None),
            P(None, "tm", "od"),
            P("tm", "od"),
            P(("tm", "od"), None),
            P(("tm", "od"), None),
            P(),
            P(),
            P(),
            P(),
        ),
        out_specs=(P("tm", None), P("tm", None)),
        check_vma=False,
    )
```

```python
import jax
import jax.numpy as jnp
from jax import lax
from jax.sharding import PartitionSpec as P
from jax.experimental import pallas as pl
from jax.experimental.pallas import tpu as pltpu

HIGHEST = lax.Precision.HIGHEST
HIGH = lax.Precision.HIGH


def joined_along(pieces, dim):
    shape = list(pieces.shape[1:])
    shape[dim] *= pieces.shape[0]
    return jnp.moveaxis(pieces, 0, dim).reshape(shape)


def from_everyone(array, axis):
    size = lax.axis_size(axis)
    return lax.all_to_all(
        jnp.broadcast_to(array[None], (size, *array.shape)), axis, 0, 0, tiled=True
    )


def collect(array, axis, dim):
    return joined_along(from_everyone(array, axis), dim)


def in_one_piece(arrays, axis, dim, along):
    widths = [a.shape[along] for a in arrays]
    both = jnp.concatenate(arrays, axis=along)
    filled = lax.all_gather(both, axis, axis=dim, tiled=True)
    return tuple(jnp.split(filled, [sum(widths[:k]) for k in range(1, len(widths))], axis=along))


def over_copies(array, axis):
    everything = from_everyone(array, axis)
    return jnp.sum(everything, axis=0)


def product(left_mat, right_mat):
    return jnp.dot(left_mat, right_mat, precision=HIGHEST)


def matrix_power(matrix, exponent):
    result = None
    squared = matrix
    while exponent > 0:
        if exponent % 2 == 1:
            result = squared
        exponent = exponent // 2
        if exponent > 0:
            squared = product(squared, squared)
    return result


def run_rows(start_state, drive, matrix, reverse):

    def advance(carried, drive_row):
        updated = jnp.dot(matrix, carried, precision=HIGHEST) + drive_row
        return (updated, updated)

    return lax.scan(advance, start_state, drive, reverse=reverse)[1]


def backward_terms(filtered, transition, smooth_gain, last_device):
    predicted = product(filtered, transition.T)
    back_terms = filtered - product(predicted, smooth_gain.T)
    row_ids = lax.broadcasted_iota(jnp.int32, back_terms.shape, 0)
    final_row = jnp.logical_and(last_device, row_ids == back_terms.shape[0] - 1)
    return jnp.where(final_row, filtered, back_terms)


def forward_start(stride, last_state):
    states = collect(last_state[None], "tm", 0)
    own_index = lax.axis_index("tm")

    def forward_horner_step(position, running):
        stepped = jnp.dot(stride, running, precision=HIGHEST) + states[position]
        return jnp.where(position < own_index, stepped, running)

    return lax.fori_loop(0, lax.axis_size("tm"), forward_horner_step, jnp.zeros_like(last_state))


def backward_start(stride, first_state):
    states = collect(first_state[None], "tm", 0)
    own_index = lax.axis_index("tm")
    group_size = lax.axis_size("tm")

    def backward_horner_step(turn, running):
        position = group_size - 1 - turn
        stepped = jnp.dot(stride, running, precision=HIGHEST) + states[position]
        return jnp.where(position > own_index, stepped, running)

    return lax.fori_loop(0, group_size, backward_horner_step, jnp.zeros_like(first_state))


def powers_of(matrices, top):
    eye = jnp.broadcast_to(jnp.eye(matrices.shape[1], dtype=matrices.dtype), matrices.shape)
    found = [eye, matrices]
    while len(found) <= top:
        reached = found[-1]
        more = jnp.einsum("pij,bpjk->bpik", reached, jnp.stack(found[1:]), precision=HIGHEST)
        found.extend(list(more))
    return jnp.stack(found[: top + 1])


def forward_sum(spread):
    rows = spread.shape[0]
    total = spread[:, 0]
    for lag in range(1, rows):
        total = total + jnp.pad(spread[: rows - lag, lag], ((lag, 0), (0, 0)))
    return total


def backward_sum(spread):
    rows = spread.shape[0]
    total = spread[:, 0]
    for lag in range(1, rows):
        total = total + jnp.pad(spread[lag:, lag], ((0, lag), (0, 0)))
    return total


def by_powers(rows_in, power_stack):
    return jnp.einsum("kr,jsr->kjs", rows_in, power_stack, precision=HIGH)


def kalman(partial_value, filter_trans, filter_gain, transition, smooth_gain):
    rows, width = partial_value.shape
    block = lax.axis_index("tm")
    blocks = lax.axis_size("tm")
    last_device = block == blocks - 1
    both_powers = powers_of(jnp.stack((filter_trans, smooth_gain)), rows)
    filter_powers = both_powers[:, 0]
    smooth_powers = both_powers[:, 1]
    both_strides = powers_of(both_powers[rows], blocks - 1)
    filter_strides = both_strides[:, 0]
    smooth_strides = both_strides[:, 1]
    eye = jnp.eye(width, dtype=jnp.float32)
    correction = eye - product(smooth_gain, transition)
    carried = jnp.einsum(
        "tij,tjk->tik",
        smooth_powers[:rows],
        jnp.einsum("ij,tjk->tik", correction, filter_powers[1:], precision=HIGH),
        precision=HIGH,
    )
    lead_map = jnp.sum(carried, axis=0)
    tail_fix = product(smooth_powers[rows - 1], product(eye - correction, filter_powers[rows]))
    last_map = lead_map + tail_fix

    observed = over_copies(partial_value, "od")
    drive = product(observed, filter_gain.T)
    zero_run = forward_sum(by_powers(drive, filter_powers[:rows]))
    zero_back = backward_terms(zero_run, transition, smooth_gain, last_device)
    zero_smooth = backward_sum(by_powers(zero_back, smooth_powers[:rows]))
    ends = collect(jnp.concatenate((zero_run[rows - 1], zero_smooth[0]))[None], "tm", 0)
    filter_ends = ends[:, :width]
    smooth_starts = ends[:, width:]

    stride_ids = lax.broadcasted_iota(jnp.int32, (blocks, blocks, blocks), 1)
    source_ids = lax.broadcasted_iota(jnp.int32, (blocks, blocks, blocks), 2)
    target_ids = lax.broadcasted_iota(jnp.int32, (blocks, blocks, blocks), 0)
    pick = (stride_ids == target_ids - 1 - source_ids).astype(jnp.float32)
    spread_ends = jnp.einsum("msr,kr->mks", filter_strides, filter_ends, precision=HIGH)
    starts = jnp.einsum("bmk,mks->bs", pick, spread_ends, precision=HIGHEST)
    block_ids = lax.broadcasted_iota(jnp.int32, (blocks, width), 0)
    through = jnp.where(
        block_ids == blocks - 1, product(starts, last_map.T), product(starts, lead_map.T)
    )
    smooth_full = smooth_starts + through
    spread_starts = jnp.einsum("msr,kr->mks", smooth_strides, smooth_full, precision=HIGH)
    mk_stride = lax.broadcasted_iota(jnp.int32, (blocks, blocks), 0)
    mk_source = lax.broadcasted_iota(jnp.int32, (blocks, blocks), 1)
    later_pick = (mk_stride == mk_source - block - 1).astype(jnp.float32)
    end_state = jnp.einsum("mk,mks->s", later_pick, spread_starts, precision=HIGHEST)
    own_pick = (lax.broadcasted_iota(jnp.int32, (blocks,), 0) == block).astype(jnp.float32)
    start_state = jnp.einsum("b,bs->s", own_pick, starts, precision=HIGHEST)

    filtered = zero_run + jnp.einsum("jsr,r->js", filter_powers[1:], start_state, precision=HIGH)
    back_terms = backward_terms(filtered, transition, smooth_gain, last_device)
    local_smooth = backward_sum(by_powers(back_terms, smooth_powers[:rows]))
    carried_end = jnp.einsum("jsr,r->js", smooth_powers[1:], end_state, precision=HIGH)
    smoothed = local_smooth + jnp.flip(carried_end, axis=0)
    return filtered, smoothed


GROUPS = (32, 16, 8, 4)


def mttkrp_kernel(coords_ref, counts_ref, tiles_ref, table_ref, out_ref, orig_ref):
    step = pl.program_id(0)
    slot_total = tiles_ref.shape[1]
    tile_side = tiles_ref.shape[2]
    state_width = orig_ref.shape[1]
    tile_top = table_ref.shape[0] // tile_side - 1

    @pl.when(step == 0)
    def _():
        orig_ref[...] = table_ref[:, pl.ds(0, state_width)].astype(jnp.float32)

    live = jnp.clip(counts_ref[step], 0, slot_total)

    def slot_term(slot):
        orig_id = jnp.clip(coords_ref[0, step, slot], 0, tile_top)
        dest_id = jnp.clip(coords_ref[1, step, slot], 0, tile_top)
        dest_start = pl.multiple_of(dest_id * tile_side, tile_side)
        orig_start = pl.multiple_of(orig_id * tile_side, tile_side)
        dest_rows = table_ref[pl.ds(dest_start, tile_side), pl.ds(state_width, state_width)]
        orig_rows = orig_ref[pl.ds(orig_start, tile_side), :]
        tile_dest = jnp.dot(tiles_ref[0, slot], dest_rows, preferred_element_type=jnp.float32)
        weighted = tile_dest * orig_rows
        return jnp.sum(weighted.reshape(tile_side // 8, 8, state_width), axis=0)

    def group_of(width, first):
        def one_group(group, acc):
            terms = [slot_term(first + group * width + k) for k in range(width)]
            while len(terms) > 1:
                terms = [terms[k] + terms[k + 1] for k in range(0, len(terms), 2)]
            return acc + terms[0]

        return one_group

    def one_slot(slot, acc):
        return acc + slot_term(slot)

    acc = jnp.zeros((8, state_width), jnp.float32)
    done = 0
    for width in GROUPS:
        groups = (live - done) // width
        acc = lax.fori_loop(0, groups, group_of(width, done), acc)
        done = done + groups * width
    acc = lax.fori_loop(done, live, one_slot, acc)
    out_ref[0] = jnp.sum(acc, axis=0, keepdims=True)


def mttkrp(tiles, coords, live_counts, table):
    step_count, slot_count, tile_side, _ = tiles.shape
    state_width = table.shape[1] // 2
    grid_spec = pltpu.PrefetchScalarGridSpec(
        num_scalar_prefetch=2,
        grid=(step_count,),
        in_specs=[
            pl.BlockSpec((1, slot_count, tile_side, tile_side), lambda t, c, n: (t, 0, 0, 0)),
            pl.BlockSpec(table.shape, lambda t, c, n: (0, 0)),
        ],
        out_specs=pl.BlockSpec((1, 1, state_width), lambda t, c, n: (t, 0, 0)),
        scratch_shapes=[pltpu.VMEM((table.shape[0], state_width), jnp.float32)],
    )
    out = pl.pallas_call(
        mttkrp_kernel,
        grid_spec=grid_spec,
        out_shape=jax.ShapeDtypeStruct((step_count, 1, state_width), jnp.float32),
        compiler_params=pltpu.CompilerParams(dimension_semantics=("arbitrary",)),
    )(coords, live_counts, tiles, table)
    return out.reshape(step_count, state_width)


def local(
    tiles,
    coords,
    counts,
    anchor_factor,
    dest_factor,
    filter_trans,
    filter_gain,
    transition,
    smooth_gain,
):
    state_width = anchor_factor.shape[1]
    table = collect(jnp.concatenate((anchor_factor, dest_factor), axis=1), ("tm", "od"), 0)
    partial_value = mttkrp(tiles, coords, counts[:, 0], table)
    return kalman(partial_value, filter_trans, filter_gain, transition, smooth_gain)


def solution(mesh):
    return jax.shard_map(
        local,
        mesh=mesh,
        in_specs=(
            P("tm", "od", None, None),
            P(None, "tm", "od"),
            P("tm", "od"),
            P(("tm", "od"), None),
            P(("tm", "od"), None),
            P(),
            P(),
            P(),
            P(),
        ),
        out_specs=(P("tm", None), P("tm", None)),
        check_vma=False,
    )
```

```python
import jax
import jax.numpy as jnp
from jax import lax
from jax.sharding import PartitionSpec as P
from jax.experimental import pallas as pl
from jax.experimental.pallas import tpu as pltpu

HIGHEST = lax.Precision.HIGHEST
HIGH = lax.Precision.HIGH


def joined_along(pieces, dim):
    shape = list(pieces.shape[1:])
    shape[dim] *= pieces.shape[0]
    return jnp.moveaxis(pieces, 0, dim).reshape(shape)


def from_everyone(array, axis):
    size = lax.axis_size(axis)
    return lax.all_to_all(
        jnp.broadcast_to(array[None], (size, *array.shape)), axis, 0, 0, tiled=True
    )


def collect(array, axis, dim):
    return joined_along(from_everyone(array, axis), dim)


def in_one_piece(arrays, axis, dim, along):
    widths = [a.shape[along] for a in arrays]
    both = jnp.concatenate(arrays, axis=along)
    filled = lax.all_gather(both, axis, axis=dim, tiled=True)
    return tuple(jnp.split(filled, [sum(widths[:k]) for k in range(1, len(widths))], axis=along))


def over_copies(array, axis):
    everything = from_everyone(array, axis)
    return jnp.sum(everything, axis=0)


def product(left_mat, right_mat):
    return jnp.dot(left_mat, right_mat, precision=HIGHEST)


def matrix_power(matrix, exponent):
    result = None
    squared = matrix
    while exponent > 0:
        if exponent % 2 == 1:
            result = squared
        exponent = exponent // 2
        if exponent > 0:
            squared = product(squared, squared)
    return result


def run_rows(start_state, drive, matrix, reverse):

    def advance(carried, drive_row):
        updated = jnp.dot(matrix, carried, precision=HIGHEST) + drive_row
        return (updated, updated)

    return lax.scan(advance, start_state, drive, reverse=reverse)[1]


def backward_terms(filtered, transition, smooth_gain, last_device):
    predicted = product(filtered, transition.T)
    back_terms = filtered - product(predicted, smooth_gain.T)
    row_ids = lax.broadcasted_iota(jnp.int32, back_terms.shape, 0)
    final_row = jnp.logical_and(last_device, row_ids == back_terms.shape[0] - 1)
    return jnp.where(final_row, filtered, back_terms)


def forward_start(stride, last_state):
    states = collect(last_state[None], "tm", 0)
    own_index = lax.axis_index("tm")

    def forward_horner_step(position, running):
        stepped = jnp.dot(stride, running, precision=HIGHEST) + states[position]
        return jnp.where(position < own_index, stepped, running)

    return lax.fori_loop(0, lax.axis_size("tm"), forward_horner_step, jnp.zeros_like(last_state))


def backward_start(stride, first_state):
    states = collect(first_state[None], "tm", 0)
    own_index = lax.axis_index("tm")
    group_size = lax.axis_size("tm")

    def backward_horner_step(turn, running):
        position = group_size - 1 - turn
        stepped = jnp.dot(stride, running, precision=HIGHEST) + states[position]
        return jnp.where(position > own_index, stepped, running)

    return lax.fori_loop(0, group_size, backward_horner_step, jnp.zeros_like(first_state))


def powers_of(matrices, top):
    eye = jnp.broadcast_to(jnp.eye(matrices.shape[1], dtype=matrices.dtype), matrices.shape)
    found = [eye, matrices]
    while len(found) <= top:
        reached = found[-1]
        more = jnp.einsum("pij,bpjk->bpik", reached, jnp.stack(found[1:]), precision=HIGHEST)
        found.extend(list(more))
    return jnp.stack(found[: top + 1])


def forward_sum(spread):
    rows = spread.shape[0]
    total = spread[:, 0]
    for lag in range(1, rows):
        total = total + jnp.pad(spread[: rows - lag, lag], ((lag, 0), (0, 0)))
    return total


def backward_sum(spread):
    rows = spread.shape[0]
    total = spread[:, 0]
    for lag in range(1, rows):
        total = total + jnp.pad(spread[lag:, lag], ((0, lag), (0, 0)))
    return total


def by_powers(rows_in, power_stack):
    return jnp.einsum("kr,jsr->kjs", rows_in, power_stack, precision=HIGH)


def kalman(partial_value, filter_trans, filter_gain, transition, smooth_gain):
    rows, width = partial_value.shape
    block = lax.axis_index("tm")
    blocks = lax.axis_size("tm")
    last_device = block == blocks - 1
    both_powers = powers_of(jnp.stack((filter_trans, smooth_gain)), rows)
    filter_powers = both_powers[:, 0]
    smooth_powers = both_powers[:, 1]
    both_strides = powers_of(both_powers[rows], blocks - 1)
    filter_strides = both_strides[:, 0]
    smooth_strides = both_strides[:, 1]
    eye = jnp.eye(width, dtype=jnp.float32)
    correction = eye - product(smooth_gain, transition)
    carried = jnp.einsum(
        "tij,tjk->tik",
        smooth_powers[:rows],
        jnp.einsum("ij,tjk->tik", correction, filter_powers[1:], precision=HIGH),
        precision=HIGH,
    )
    lead_map = jnp.sum(carried, axis=0)
    tail_fix = product(smooth_powers[rows - 1], product(eye - correction, filter_powers[rows]))
    last_map = lead_map + tail_fix

    observed = over_copies(partial_value, "od")
    drive = product(observed, filter_gain.T)
    zero_run = forward_sum(by_powers(drive, filter_powers[:rows]))
    zero_back = backward_terms(zero_run, transition, smooth_gain, last_device)
    zero_smooth = backward_sum(by_powers(zero_back, smooth_powers[:rows]))
    ends = collect(jnp.concatenate((zero_run[rows - 1], zero_smooth[0]))[None], "tm", 0)
    filter_ends = ends[:, :width]
    smooth_starts = ends[:, width:]

    stride_ids = lax.broadcasted_iota(jnp.int32, (blocks, blocks, blocks), 1)
    source_ids = lax.broadcasted_iota(jnp.int32, (blocks, blocks, blocks), 2)
    target_ids = lax.broadcasted_iota(jnp.int32, (blocks, blocks, blocks), 0)
    pick = (stride_ids == target_ids - 1 - source_ids).astype(jnp.float32)
    spread_ends = jnp.einsum("msr,kr->mks", filter_strides, filter_ends, precision=HIGH)
    starts = jnp.einsum("bmk,mks->bs", pick, spread_ends, precision=HIGHEST)
    block_ids = lax.broadcasted_iota(jnp.int32, (blocks, width), 0)
    through = jnp.where(
        block_ids == blocks - 1, product(starts, last_map.T), product(starts, lead_map.T)
    )
    smooth_full = smooth_starts + through
    spread_starts = jnp.einsum("msr,kr->mks", smooth_strides, smooth_full, precision=HIGH)
    mk_stride = lax.broadcasted_iota(jnp.int32, (blocks, blocks), 0)
    mk_source = lax.broadcasted_iota(jnp.int32, (blocks, blocks), 1)
    later_pick = (mk_stride == mk_source - block - 1).astype(jnp.float32)
    end_state = jnp.einsum("mk,mks->s", later_pick, spread_starts, precision=HIGHEST)
    own_pick = (lax.broadcasted_iota(jnp.int32, (blocks,), 0) == block).astype(jnp.float32)
    start_state = jnp.einsum("b,bs->s", own_pick, starts, precision=HIGHEST)

    filtered = zero_run + jnp.einsum("jsr,r->js", filter_powers[1:], start_state, precision=HIGH)
    back_terms = backward_terms(filtered, transition, smooth_gain, last_device)
    local_smooth = backward_sum(by_powers(back_terms, smooth_powers[:rows]))
    carried_end = jnp.einsum("jsr,r->js", smooth_powers[1:], end_state, precision=HIGH)
    smoothed = local_smooth + jnp.flip(carried_end, axis=0)
    return filtered, smoothed


GROUPS = (32, 16, 8, 4)


def mttkrp_kernel(coords_ref, counts_ref, tiles_ref, table_ref, out_ref, orig_ref):
    step = pl.program_id(0)
    slot_total = tiles_ref.shape[1]
    tile_side = tiles_ref.shape[2]
    state_width = orig_ref.shape[1]
    tile_top = table_ref.shape[0] // tile_side - 1

    @pl.when(step == 0)
    def _():
        orig_ref[...] = table_ref[:, pl.ds(0, state_width)].astype(jnp.float32)

    live = jnp.clip(counts_ref[step], 0, slot_total)

    def slot_term(slot):
        slot = jnp.minimum(slot, slot_total - 1)
        orig_id = jnp.clip(coords_ref[0, step, slot], 0, tile_top)
        dest_id = jnp.clip(coords_ref[1, step, slot], 0, tile_top)
        dest_start = pl.multiple_of(dest_id * tile_side, tile_side)
        orig_start = pl.multiple_of(orig_id * tile_side, tile_side)
        dest_rows = table_ref[pl.ds(dest_start, tile_side), pl.ds(state_width, state_width)]
        orig_rows = orig_ref[pl.ds(orig_start, tile_side), :]
        tile_dest = jnp.dot(tiles_ref[0, slot], dest_rows, preferred_element_type=jnp.float32)
        weighted = tile_dest * orig_rows
        return jnp.sum(weighted.reshape(tile_side // 8, 8, state_width), axis=0)

    def group_of(width, first):
        def one_group(group, acc):
            terms = [slot_term(first + group * width + k) for k in range(width)]
            while len(terms) > 1:
                terms = [terms[k] + terms[k + 1] for k in range(0, len(terms), 2)]
            return acc + terms[0]

        return one_group

    def one_slot(slot, acc):
        return acc + slot_term(slot)

    acc = jnp.zeros((8, state_width), jnp.float32)
    done = 0
    for width in GROUPS:
        groups = (live - done) // width
        acc = lax.fori_loop(0, groups, group_of(width, done), acc)
        done = done + groups * width
    def last_group(unused, acc):
        terms = [
            jnp.where(done + k < live, slot_term(done + k), 0.0) for k in range(GROUPS[-1])
        ]
        while len(terms) > 1:
            terms = [terms[k] + terms[k + 1] for k in range(0, len(terms), 2)]
        return acc + terms[0]

    acc = lax.fori_loop(0, jnp.minimum(live - done, 1), last_group, acc)
    out_ref[0] = jnp.sum(acc, axis=0, keepdims=True)


def mttkrp(tiles, coords, live_counts, table):
    step_count, slot_count, tile_side, _ = tiles.shape
    state_width = table.shape[1] // 2
    grid_spec = pltpu.PrefetchScalarGridSpec(
        num_scalar_prefetch=2,
        grid=(step_count,),
        in_specs=[
            pl.BlockSpec((1, slot_count, tile_side, tile_side), lambda t, c, n: (t, 0, 0, 0)),
            pl.BlockSpec(table.shape, lambda t, c, n: (0, 0)),
        ],
        out_specs=pl.BlockSpec((1, 1, state_width), lambda t, c, n: (t, 0, 0)),
        scratch_shapes=[pltpu.VMEM((table.shape[0], state_width), jnp.float32)],
    )
    out = pl.pallas_call(
        mttkrp_kernel,
        grid_spec=grid_spec,
        out_shape=jax.ShapeDtypeStruct((step_count, 1, state_width), jnp.float32),
        compiler_params=pltpu.CompilerParams(dimension_semantics=("arbitrary",)),
    )(coords, live_counts, tiles, table)
    return out.reshape(step_count, state_width)


def local(
    tiles,
    coords,
    counts,
    anchor_factor,
    dest_factor,
    filter_trans,
    filter_gain,
    transition,
    smooth_gain,
):
    state_width = anchor_factor.shape[1]
    table = collect(jnp.concatenate((anchor_factor, dest_factor), axis=1), ("tm", "od"), 0)
    partial_value = mttkrp(tiles, coords, counts[:, 0], table)
    return kalman(partial_value, filter_trans, filter_gain, transition, smooth_gain)


def solution(mesh):
    return jax.shard_map(
        local,
        mesh=mesh,
        in_specs=(
            P("tm", "od", None, None),
            P(None, "tm", "od"),
            P("tm", "od"),
            P(("tm", "od"), None),
            P(("tm", "od"), None),
            P(),
            P(),
            P(),
            P(),
        ),
        out_specs=(P("tm", None), P("tm", None)),
        check_vma=False,
    )
```
